256 devices in a mesh: dp: 16 (over z, core), expert: 16 (over y, x).
Axes of the slice: x: 4, y: 4, z: 8, core: 2. Of those that a mesh axis runs over, the one named last changes fastest.
Arguments:
- queries: bfloat16 [34816, 1536], P(('dp', 'expert')), may hold values from -6 to 6
- fresh_keys: bfloat16 [34816, 256], P(('dp', 'expert')), may hold values from -1 to 1
- fresh_values: bfloat16 [34816, 256], P(('dp', 'expert')), may hold values from -6 to 6
- residual: bfloat16 [34816, 1536], P(('dp', 'expert')), may hold values from -6 to 6
- norm_gain: float32 [1536], replicated, may hold values from 0.25 to 1.75
- out_weight: bfloat16 [1536, 1536], replicated, may hold values from -0.15625 to 0.15625
- router_weight: bfloat16 [1536, 16], replicated, may hold values from -0.15625 to 0.15625
- gate_weight: bfloat16 [16, 1536, 384], P('expert'), may hold values from -0.15625 to 0.15625
- up_weight: bfloat16 [16, 1536, 384], P('expert'), may hold values from -0.15625 to 0.15625
- down_weight: bfloat16 [16, 384, 1536], P('expert'), may hold values from -0.3125 to 0.3125
- expert_ids: int32 [34816, 4], P(('dp', 'expert')), may hold values from 0 to 15, all different within a row; in each aligned block of 136 rows (0 to 135, 136 to 271, ...) at most 56 rows name the same one
- paged_keys: bfloat16 [3072, 128, 256], P(('dp', 'expert')), may hold values from -1 to 1
- paged_values: bfloat16 [3072, 128, 256], P(('dp', 'expert')), may hold values from -6 to 6
- decode_table: int32 [1792, 4], P(('dp', 'expert')), may hold values from 0 to 11
- prefill_table: int32 [256, 4], P(('dp', 'expert')), may hold values from 0 to 11
- decode_len: int32 [256, 8], P(('dp', 'expert')), may hold values from 1 to 511, 2048 in all within a row
- prefill_len: int32 [256], P(('dp', 'expert')), may hold values from 0 to 512
- departing_keys: bfloat16 [256, 512, 256], P(('dp', 'expert')), may hold values from -1 to 1
- departing_values: bfloat16 [256, 512, 256], P(('dp', 'expert')), may hold values from -6 to 6
- destination: int32 [16, 16], P('expert'), may hold values from 0 to 15, each once within a row
Outputs:
- layer_out: bfloat16 [34816, 1536], P(('dp', 'expert'))
- moved_keys: bfloat16 [256, 512, 256], P(('dp', 'expert'))
- moved_values: bfloat16 [256, 512, 256], P(('dp', 'expert'))
The draws below stay inside these ranges and needn't reach their ends.
Inputs may be any that keep to these rules, and one draw needn't show every extreme that they name: `expert_ids`: in each device's 136 rows no expert is named by more than 56 rows, a bound that some block reaches. `decode_len`: each device's 8 lengths sum to 2048 and the largest is 511. `destination`: each row is a permutation of the dp indices. `decode_table`: entries index pages of the device's own pool. `prefill_table`: entries index pages of the device's own pool.
All inputs are finite; a program needn't handle non-finite values.
Results may differ from the reference program's by a relative error of at most 0.0045.
Values may be sent and summed in bfloat16 or wider, within the bound.
No kernel may reach another device: no remote copies, remote signals or barrier semaphores. Data moves between devices by JAX's collectives and lax.ppermute only.
A program may use at most 128 MiB of HBM per device.

```python
import math
import jax
import jax.numpy as jnp
import numpy as np
from jax import lax

D = 1536
QUERY_HEADS = 12
KEY_VALUE_HEADS = 2
HEAD_SIZE = 128
FF = 384
TOPK = 4
PAGE_TOKENS = 128
MAXP = 4
POOL_PAGES = 12
DEC_DEV = 8
PCH = 128
E = 16
CONTEXT_LENGTH = 512
DEVICE_TOKENS = 136
CAP = 56
N_DP = 16
N_EXPERT = 16
DEVICES = 256


def plant(values, key, low, high):
    index_at = [jax.random.randint(jax.random.fold_in(key, axis), (), 0, length) for axis, length in enumerate(values.shape)]
    main_axis = values.shape.index(max(values.shape))
    beside = index_at[:main_axis] + [(index_at[main_axis] + 1) % values.shape[main_axis]] + index_at[main_axis + 1:]
    return values.at[tuple(index_at)].set(low).at[tuple(beside)].set(high)


def block_scale(rng, extent, cuts, smallest, high):
    gain = 1.0
    for axis_at, shards_of in cuts:
        draws = jax.random.uniform(jax.random.fold_in(jax.random.fold_in(rng, 6), axis_at), (shards_of,), jnp.float32, smallest / len(cuts), high / len(cuts))
        gain = gain * jnp.repeat(jnp.exp(draws), extent[axis_at] // shards_of).reshape((-1,) + (1,) * (len(extent) - 1 - axis_at))
    return gain


def length_profile(count, total, limit, skew):
    loads = [(1 << 20) // math.isqrt(standing ** skew) + 1 for standing in range(2, count + 1)]
    spare, counts = total - limit - (count - 1), [1] * (count - 1)
    while spare > 0:
        movable = [i for i in range(count - 1) if counts[i] < limit]
        pool, remaining = sum([loads[i] for i in movable]), spare
        for i in movable:
            addition = min(limit - counts[i], max(1, remaining * loads[i] // pool), spare)
            counts[i] = counts[i] + addition
            spare = spare - addition
    return np.array([limit] + counts)


def uneven_parts(own_key, count, total, limit, lean):
    if count == 2:
        one = jax.random.randint(own_key, (), max(1, total - limit), min(limit, total - 1) + 1)
        return jnp.stack([one, total - one])
    tallies = jnp.asarray(length_profile(count, total, limit, lean), jnp.int32)
    twos = (count - 1) // 2
    giver, receiver = tallies[1:1 + 2 * twos:2], tallies[2:2 + 2 * twos:2]
    room = jnp.minimum(giver - 1, limit - receiver)
    moved = jax.random.randint(jax.random.fold_in(own_key, 1), (twos,), 0, 1 << 20) % (room + 1)
    tallies = tallies.at[1:1 + 2 * twos:2].set(giver - moved).at[2:2 + 2 * twos:2].set(receiver + moved)
    return tallies[jax.random.permutation(jax.random.fold_in(own_key, 2), count)]


def deal_out(rng, own, number, rows, amount, top, bound, skew):
    order = jax.random.permutation(rng, amount)
    heavy_load, common = shares(amount, rows * top, bound, skew, True), shares(amount, rows * top, bound, skew, False)
    places = jnp.arange(amount)

    def named(sizes, offset_by):
        used = int((sizes > 0).sum())
        fixed = max(1, used // 4)
        passed = fixed + (places - fixed + offset_by * (used - fixed)) % max(1, amount - fixed)
        return jnp.zeros((amount,), jnp.int32).at[order[jnp.where(places < fixed, places, passed)]].set(jnp.asarray(sizes, jnp.int32))

    sizes = jnp.where(number % 4 == 0, named(heavy_load, number // 4), named(common, number - number // 4 - 1))
    mixed = jax.random.permutation(jax.random.fold_in(own, 3), amount)
    donor, sink = mixed[0:amount // 2 * 2:2], mixed[1:amount // 2 * 2:2]
    slack = jnp.minimum(sizes[donor] - 1, bound - sizes[sink]) // 2
    slack = jnp.where((donor == order[0]) | (sink == order[0]) | (sizes[sink] == 0), 0, jnp.maximum(slack, 0))
    passed = jax.random.randint(jax.random.fold_in(own, 4), (amount // 2,), 0, 1 << 20) % (slack + 1)
    sizes = sizes.at[donor].add(-passed).at[sink].add(passed)
    labels = jnp.searchsorted(jnp.cumsum(sizes), jnp.arange(rows * top), side="right").astype(jnp.int32)
    table = labels.reshape(top, rows).T
    table = table[jax.random.permutation(jax.random.fold_in(own, 1), rows)]
    offset_by = jax.random.randint(jax.random.fold_in(own, 2), (rows, 1), 0, top)
    return jnp.take_along_axis(table, (jnp.arange(top)[None, :] + offset_by) % top, axis=1)


def shares(amount, total, bound, skew, full):
    weights = [(1 << 20) // math.isqrt(grade ** skew) + 1 for grade in range(1, amount + 1)]
    largest = bound if full else min(bound, max(-(-total // amount), total * weights[0] // sum(weights)))
    least = 1 if total - largest >= amount - 1 else 0
    holding, surplus = [largest] + [least] * (amount - 1), total - largest - least * (amount - 1)
    while surplus > 0:
        candidates = [i for i in range(1, amount) if holding[i] < largest] or [i for i in range(1, amount) if holding[i] < bound]
        mass, budget = sum([weights[i] for i in candidates]), surplus
        for i in candidates:
            more = min(bound - holding[i], max(1, budget * weights[i] // mass), surplus)
            holding[i] = holding[i] + more
            surplus = surplus - more
    return np.array(holding)


def noise(rng, extent, deviation, reach, pieces=(), held_as=jnp.bfloat16):
    drawn = deviation * jax.random.normal(rng, extent, jnp.float32)
    if pieces:
        drawn = drawn * block_scale(rng, extent, pieces, -0.22, 0.18)
    return jnp.clip(drawn, -reach, reach).astype(held_as)


def setup_inputs(seed: int = 0) -> dict:
    streams_of = jax.random.split(jax.random.key(seed), 21)
    queries = noise(streams_of[0], (DEVICES * DEVICE_TOKENS, QUERY_HEADS * HEAD_SIZE), 1.0, 6.0, ((0, 256),))
    fresh_keys = jnp.clip(jax.random.uniform(streams_of[1], (DEVICES * DEVICE_TOKENS, KEY_VALUE_HEADS * HEAD_SIZE), jnp.float32, -1.0, 1.0) * block_scale(streams_of[1], (DEVICES * DEVICE_TOKENS, KEY_VALUE_HEADS * HEAD_SIZE), ((0, 256),), -0.4, 0.0), -1.0, 1.0).astype(jnp.bfloat16)
    fresh_values = noise(streams_of[2], (DEVICES * DEVICE_TOKENS, KEY_VALUE_HEADS * HEAD_SIZE), 1.0, 6.0, ((0, 256),))
    residual = noise(streams_of[3], (DEVICES * DEVICE_TOKENS, D), 1.0, 6.0, ((0, 256),))
    norm_gain = jnp.clip(1.0 + 0.15 * jax.random.normal(streams_of[4], (D,), jnp.float32), 0.25, 1.75)
    out_weight = noise(streams_of[5], (QUERY_HEADS * HEAD_SIZE, D), (QUERY_HEADS * HEAD_SIZE) ** -0.5, 0.15625)
    router_weight = noise(streams_of[6], (D, E), D ** -0.5, 0.15625)
    gate_weight = noise(streams_of[7], (E, D, FF), D ** -0.5, 0.15625, ((0, 16),))
    up_weight = noise(streams_of[8], (E, D, FF), D ** -0.5, 0.15625, ((0, 16),))
    down_weight = noise(streams_of[9], (E, FF, D), FF ** -0.5, 0.3125, ((0, 16),))
    expert_ids_keys = jax.random.split(jax.random.fold_in(streams_of[10], 1), (DEVICES * DEVICE_TOKENS) // DEVICE_TOKENS)
    expert_ids_turns = jax.random.permutation(jax.random.fold_in(streams_of[10], 3), (DEVICES * DEVICE_TOKENS) // DEVICE_TOKENS)
    expert_ids = jax.vmap(lambda own, number: deal_out(jax.random.fold_in(streams_of[10], 2), own, number, DEVICE_TOKENS, E, TOPK, CAP, 2))(expert_ids_keys, expert_ids_turns).reshape((DEVICES * DEVICE_TOKENS, TOPK))
    paged_keys = jnp.clip(jax.random.uniform(streams_of[11], (DEVICES * POOL_PAGES, PAGE_TOKENS, KEY_VALUE_HEADS * HEAD_SIZE), jnp.float32, -1.0, 1.0) * block_scale(streams_of[11], (DEVICES * POOL_PAGES, PAGE_TOKENS, KEY_VALUE_HEADS * HEAD_SIZE), ((0, 256),), -0.4, 0.0), -1.0, 1.0).astype(jnp.bfloat16)
    paged_values = noise(streams_of[12], (DEVICES * POOL_PAGES, PAGE_TOKENS, KEY_VALUE_HEADS * HEAD_SIZE), 1.0, 6.0, ((0, 256),))
    decode_table = plant(jax.random.randint(streams_of[13], (DEVICES * (DEC_DEV - 1), MAXP), 0, POOL_PAGES), jax.random.fold_in(streams_of[13], 1), 0, POOL_PAGES - 1).astype(jnp.int32)
    prefill_table = plant(jax.random.randint(streams_of[14], (DEVICES, MAXP), 0, POOL_PAGES), jax.random.fold_in(streams_of[14], 1), 0, POOL_PAGES - 1).astype(jnp.int32)
    decode_len = jax.vmap(lambda own: uneven_parts(own, DEC_DEV, DEC_DEV * CONTEXT_LENGTH // 2, CONTEXT_LENGTH - 1, 2))(jax.random.split(streams_of[15], DEVICES)).reshape((DEVICES, DEC_DEV)).astype(jnp.int32)
    prefill_len = plant(jax.random.randint(streams_of[16], (DEVICES,), 0, CONTEXT_LENGTH + 1), jax.random.fold_in(streams_of[16], 1), 0, CONTEXT_LENGTH).astype(jnp.int32)
    departing_keys = jnp.clip(jax.random.uniform(streams_of[17], (DEVICES, CONTEXT_LENGTH, KEY_VALUE_HEADS * HEAD_SIZE), jnp.float32, -1.0, 1.0) * block_scale(streams_of[17], (DEVICES, CONTEXT_LENGTH, KEY_VALUE_HEADS * HEAD_SIZE), ((0, 256),), -0.4, 0.0), -1.0, 1.0).astype(jnp.bfloat16)
    departing_values = noise(streams_of[18], (DEVICES, CONTEXT_LENGTH, KEY_VALUE_HEADS * HEAD_SIZE), 1.0, 6.0, ((0, 256),))
    destination = jax.vmap(lambda own: jax.random.permutation(own, N_DP))(jax.random.split(streams_of[19], N_EXPERT)).reshape((N_EXPERT, N_DP)).astype(jnp.int32)
    return dict(queries=queries, fresh_keys=fresh_keys, fresh_values=fresh_values, residual=residual, norm_gain=norm_gain, out_weight=out_weight, router_weight=router_weight, gate_weight=gate_weight, up_weight=up_weight, down_weight=down_weight, expert_ids=expert_ids, paged_keys=paged_keys, paged_values=paged_values, decode_table=decode_table, prefill_table=prefill_table, decode_len=decode_len, prefill_len=prefill_len, departing_keys=departing_keys, departing_values=departing_values, destination=destination)


def attend(query_row_block, key_row_block, value_row_block, valid):
    batch_groups = query_row_block.shape[0]
    query_total = query_row_block.shape[1]
    key_total = key_row_block.shape[1]
    grouped_rows = query_row_block.reshape(batch_groups, query_total, KEY_VALUE_HEADS, QUERY_HEADS // KEY_VALUE_HEADS, HEAD_SIZE).astype(jnp.float32)
    key_head_rows = key_row_block.reshape(batch_groups, key_total, KEY_VALUE_HEADS, HEAD_SIZE).astype(jnp.float32)
    value_head_rows = value_row_block.reshape(batch_groups, key_total, KEY_VALUE_HEADS, HEAD_SIZE).astype(jnp.float32)
    scores = jnp.einsum('bqhgd,bkhd->bqhgk', grouped_rows, key_head_rows) * HEAD_SIZE ** (-0.5)
    weights = jnp.where(valid[:, :, None, None, :], jnp.exp(scores), 0.0)
    totals = lax.optimization_barrier(jnp.sum(weights, axis=-1))
    rounded = lax.optimization_barrier(weights.astype(jnp.bfloat16)).astype(jnp.float32)
    mixed = jnp.einsum('bqhgk,bkhd->bqhgd', rounded, value_head_rows) / totals[..., None]
    return mixed.reshape(batch_groups, query_total, QUERY_HEADS * HEAD_SIZE).astype(jnp.bfloat16)

def device_attention(operands):
    queries, fresh_keys, fresh_values, paged_keys, paged_values, decode_table, prefill_table, decode_len, prefill_len, arrived_keys, arrived_values = operands
    width_total = KEY_VALUE_HEADS * HEAD_SIZE
    resident_keys = paged_keys[decode_table].reshape(DEC_DEV - 1, CONTEXT_LENGTH, width_total)
    resident_values = paged_values[decode_table].reshape(DEC_DEV - 1, CONTEXT_LENGTH, width_total)
    cache_keys = jnp.concatenate([resident_keys, arrived_keys[None]], axis=0)
    cache_values = jnp.concatenate([resident_values, arrived_values[None]], axis=0)
    decode_keys = jnp.concatenate([cache_keys, fresh_keys[:DEC_DEV, None]], axis=1)
    decode_values = jnp.concatenate([cache_values, fresh_values[:DEC_DEV, None]], axis=1)
    positions = jnp.arange(CONTEXT_LENGTH, dtype=jnp.int32)
    decode_valid = jnp.concatenate([positions[None, :] < decode_len[:, None], jnp.ones((DEC_DEV, 1), dtype=bool)], axis=1)[:, None, :]
    decode_out = attend(queries[:DEC_DEV, None], decode_keys, decode_values, decode_valid)[:, 0]
    context_keys = paged_keys[prefill_table].reshape(CONTEXT_LENGTH, width_total)
    context_values = paged_values[prefill_table].reshape(CONTEXT_LENGTH, width_total)
    block_keys = jnp.concatenate([context_keys, fresh_keys[DEC_DEV:]], axis=0)[None]
    block_values = jnp.concatenate([context_values, fresh_values[DEC_DEV:]], axis=0)[None]
    block_pos = jnp.arange(PCH, dtype=jnp.int32)
    context_valid = jnp.broadcast_to(positions[None, :] < prefill_len, (PCH, CONTEXT_LENGTH))
    causal = block_pos[None, :] <= block_pos[:, None]
    block_valid = jnp.concatenate([context_valid, causal], axis=1)[None]
    block_out = attend(queries[DEC_DEV:][None], block_keys, block_values, block_valid)[0]
    return jnp.concatenate([decode_out, block_out], axis=0)

def reference(queries, fresh_keys, fresh_values, residual, norm_gain, out_weight, router_weight, gate_weight, up_weight, down_weight, expert_ids, paged_keys, paged_values, decode_table, prefill_table, decode_len, prefill_len, departing_keys, departing_values, destination):
    device_count = N_DP * N_EXPERT
    width_total = KEY_VALUE_HEADS * HEAD_SIZE
    device_ids = jnp.arange(device_count, dtype=jnp.int32)
    column = device_ids % N_EXPERT
    targets = destination[column, device_ids // N_EXPERT] * N_EXPERT + column
    arrived_keys = jnp.zeros_like(departing_keys).at[targets].set(departing_keys)
    arrived_values = jnp.zeros_like(departing_values).at[targets].set(departing_values)
    operands = (queries.reshape(device_count, DEVICE_TOKENS, QUERY_HEADS * HEAD_SIZE), fresh_keys.reshape(device_count, DEVICE_TOKENS, width_total), fresh_values.reshape(device_count, DEVICE_TOKENS, width_total), paged_keys.reshape(device_count, POOL_PAGES, PAGE_TOKENS, width_total), paged_values.reshape(device_count, POOL_PAGES, PAGE_TOKENS, width_total), decode_table.reshape(device_count, DEC_DEV - 1, MAXP), prefill_table, decode_len, prefill_len, arrived_keys, arrived_values)
    attended = lax.map(device_attention, operands).reshape(device_count * DEVICE_TOKENS, QUERY_HEADS * HEAD_SIZE)
    hidden = residual.astype(jnp.float32) + jnp.dot(attended, out_weight, preferred_element_type=jnp.float32)
    variance = lax.optimization_barrier(jnp.mean(hidden * hidden, axis=-1, keepdims=True))
    normed = (hidden * lax.rsqrt(variance + 1e-06) * norm_gain).astype(jnp.bfloat16)
    logits = jnp.dot(normed, router_weight, preferred_element_type=jnp.float32)
    chosen = jax.nn.sigmoid(jnp.take_along_axis(logits, expert_ids, axis=1))
    gates = chosen / lax.optimization_barrier(jnp.sum(chosen, axis=1, keepdims=True))
    flat_ids = expert_ids.reshape(-1)
    flat_gates = gates.reshape(-1)
    slots = device_count * CAP

    def expert_step(accum, operand):
        gate_mat, up_mat, down_mat, expert_index = operand
        hits = flat_ids == expert_index
        route_rows = jnp.nonzero(hits, size=slots, fill_value=0)[0]
        live = jnp.arange(slots) < jnp.sum(hits.astype(jnp.int32))
        token_rows = route_rows // TOPK
        gathered = normed[token_rows]
        gate_part = jnp.dot(gathered, gate_mat, preferred_element_type=jnp.float32)
        up_part = jnp.dot(gathered, up_mat, preferred_element_type=jnp.float32)
        inner = (jax.nn.relu(gate_part) * up_part).astype(jnp.bfloat16)
        expert_out = jnp.dot(inner, down_mat, preferred_element_type=jnp.float32).astype(jnp.bfloat16)
        factor = jnp.where(live, flat_gates[route_rows], 0.0)
        accum = accum.at[token_rows].add(factor[:, None] * expert_out.astype(jnp.float32))
        return (accum, None)
    mixture, _ = lax.scan(expert_step, jnp.zeros(hidden.shape, jnp.float32), (gate_weight, up_weight, down_weight, jnp.arange(E, dtype=jnp.int32)))
    layer_out = (hidden + mixture).astype(jnp.bfloat16)
    new_rows = DEC_DEV - 1 + jnp.arange(device_count, dtype=jnp.int32) * DEVICE_TOKENS
    last_keys = fresh_keys[new_rows]
    last_values = fresh_values[new_rows]
    last_len = decode_len[:, DEC_DEV - 1]

    def write_row(cache, row, where_at):
        return lax.dynamic_update_slice(cache, row[None], (where_at, jnp.zeros((), jnp.int32)))
    moved_keys = jax.vmap(write_row)(arrived_keys, last_keys, last_len)
    moved_values = jax.vmap(write_row)(arrived_values, last_values, last_len)
    return (layer_out, moved_keys, moved_values)
```

```python
import jax
import jax.numpy as jnp
from jax import lax
from jax.sharding import PartitionSpec as P

QUERY_HEADS = 12
KEY_VALUE_HEADS = 2
HEAD_SIZE = 128
DEC_DEV = 8
PCH = 128
CONTEXT_LENGTH = 512


def attend(query_row_block, key_row_block, value_row_block, valid):
    batch_groups = query_row_block.shape[0]
    query_total = query_row_block.shape[1]
    key_total = key_row_block.shape[1]
    grouped_rows = query_row_block.reshape(
        batch_groups, query_total, KEY_VALUE_HEADS, QUERY_HEADS // KEY_VALUE_HEADS, HEAD_SIZE
    )
    key_head_rows = key_row_block.reshape(batch_groups, key_total, KEY_VALUE_HEADS, HEAD_SIZE)
    value_head_rows = value_row_block.reshape(batch_groups, key_total, KEY_VALUE_HEADS, HEAD_SIZE)
    scores = jnp.einsum(
        "bqhgd,bkhd->bqhgk", grouped_rows, key_head_rows, preferred_element_type=jnp.float32
    ) * HEAD_SIZE ** (-0.5)
    weights = jnp.where(valid[:, :, None, None, :], jnp.exp(scores), 0.0)
    totals = jnp.sum(weights, axis=-1)
    mixed = (
        jnp.einsum(
            "bqhgk,bkhd->bqhgd",
            weights.astype(jnp.bfloat16),
            value_head_rows,
            preferred_element_type=jnp.float32,
        )
        / totals[..., None]
    )
    return mixed.reshape(batch_groups, query_total, QUERY_HEADS * HEAD_SIZE).astype(jnp.bfloat16)


def capacity_for(token_count, route_count, expert_count):
    return min(token_count, (token_count * route_count // expert_count * 3 // 2 + 7) // 8 * 8)


def page_lookup(table, pool_flat):
    pool_count = pool_flat.shape[0]
    selector = (table[..., None] == jnp.arange(pool_count, dtype=jnp.int32)).astype(jnp.bfloat16)
    return jnp.einsum(
        "...p,pk->...k", selector, pool_flat, preferred_element_type=jnp.float32
    ).astype(jnp.bfloat16)


def on_device(
    queries,
    fresh_keys,
    fresh_values,
    residual,
    norm_gain,
    out_weight,
    router_weight,
    gate_weight,
    up_weight,
    down_weight,
    expert_ids,
    paged_keys,
    paged_values,
    decode_table,
    prefill_table,
    decode_len,
    prefill_len,
    departing_keys,
    departing_values,
    destination,
):
    width_total = KEY_VALUE_HEADS * HEAD_SIZE
    target_row = destination[0]
    dp_count = target_row.shape[0]
    rows_total = departing_keys.shape[1]
    chunk_rows = rows_total // dp_count
    both = jnp.concatenate([departing_keys[0], departing_values[0]], axis=-1)
    both = both.reshape(dp_count, chunk_rows, 2 * width_total)
    spread = lax.all_to_all(both, "dp", split_axis=0, concat_axis=0, tiled=True)
    sources = jnp.sum(
        jnp.where(
            target_row[None, :] == jnp.arange(dp_count, dtype=jnp.int32)[:, None],
            jnp.arange(dp_count, dtype=jnp.int32)[None, :],
            0,
        ),
        axis=1,
    )
    routed = jnp.take(spread, sources, axis=0)
    gathered = lax.all_to_all(routed, "dp", split_axis=0, concat_axis=0, tiled=True)
    gathered = gathered.reshape(rows_total, 2 * width_total)
    take_keys = gathered[None, :, :width_total]
    take_values = gathered[None, :, width_total:]
    pool_count = paged_keys.shape[0]
    page_rows = paged_keys.shape[1]
    pool_key_flat = paged_keys.reshape(pool_count, page_rows * width_total)
    pool_value_flat = paged_values.reshape(pool_count, page_rows * width_total)
    resident_keys = page_lookup(decode_table, pool_key_flat).reshape(
        DEC_DEV - 1, CONTEXT_LENGTH, width_total
    )
    resident_values = page_lookup(decode_table, pool_value_flat).reshape(
        DEC_DEV - 1, CONTEXT_LENGTH, width_total
    )
    decode_keys = jnp.concatenate(
        [jnp.concatenate([resident_keys, take_keys], axis=0), fresh_keys[:DEC_DEV, None]], axis=1
    )
    decode_values = jnp.concatenate(
        [jnp.concatenate([resident_values, take_values], axis=0), fresh_values[:DEC_DEV, None]],
        axis=1,
    )
    positions = jnp.arange(CONTEXT_LENGTH, dtype=jnp.int32)
    decode_valid = jnp.concatenate(
        [positions[None, :] < decode_len[0][:, None], jnp.ones((DEC_DEV, 1), dtype=bool)], axis=1
    )[:, None, :]
    decode_out = attend(queries[:DEC_DEV, None], decode_keys, decode_values, decode_valid)[:, 0]
    context_keys = page_lookup(prefill_table[0], pool_key_flat).reshape(CONTEXT_LENGTH, width_total)
    context_values = page_lookup(prefill_table[0], pool_value_flat).reshape(
        CONTEXT_LENGTH, width_total
    )
    block_keys = jnp.concatenate([context_keys, fresh_keys[DEC_DEV:]], axis=0)[None]
    block_values = jnp.concatenate([context_values, fresh_values[DEC_DEV:]], axis=0)[None]
    block_pos = jnp.arange(PCH, dtype=jnp.int32)
    context_valid = jnp.broadcast_to(positions[None, :] < prefill_len[0], (PCH, CONTEXT_LENGTH))
    causal = block_pos[None, :] <= block_pos[:, None]
    block_valid = jnp.concatenate([context_valid, causal], axis=1)[None]
    block_out = attend(queries[DEC_DEV:][None], block_keys, block_values, block_valid)[0]
    attended = jnp.concatenate([decode_out, block_out], axis=0)
    hidden = residual.astype(jnp.float32) + jnp.dot(
        attended, out_weight, preferred_element_type=jnp.float32
    )
    variance = jnp.mean(hidden * hidden, axis=-1, keepdims=True)
    normed = (hidden * lax.rsqrt(variance + 1e-06) * norm_gain).astype(jnp.bfloat16)
    logits = jnp.dot(normed, router_weight, preferred_element_type=jnp.float32)
    expert_count = router_weight.shape[1]
    expert_range = jnp.arange(expert_count, dtype=jnp.int32)
    chosen = jnp.sum(
        jnp.where(expert_ids[:, :, None] == expert_range, logits[:, None, :], 0.0), axis=-1
    )
    chosen = jax.nn.sigmoid(chosen)
    gates = chosen / jnp.sum(chosen, axis=1, keepdims=True)
    token_count = expert_ids.shape[0]
    route_count = expert_ids.shape[1]
    capacity = capacity_for(token_count, route_count, expert_count)
    slot_total = expert_count * capacity
    flat_ids = expert_ids.reshape(-1)
    hits = (flat_ids[:, None] == expert_range[None, :]).astype(jnp.int32)
    ranks = jnp.sum((jnp.cumsum(hits, axis=0) - 1) * hits, axis=1)
    slot_of_route = flat_ids * capacity + ranks
    route_slots = (
        slot_of_route[:, None] == jnp.arange(slot_total, dtype=jnp.int32)[None, :]
    ).astype(jnp.bfloat16)
    token_slots = jnp.sum(route_slots.reshape(token_count, route_count, slot_total), axis=1)
    outgoing = jnp.einsum(
        "ts,td->sd", token_slots, normed, preferred_element_type=jnp.float32
    ).astype(jnp.bfloat16)
    outgoing = outgoing.reshape(expert_count, capacity, normed.shape[1])
    received = lax.all_to_all(outgoing, "expert", split_axis=0, concat_axis=0, tiled=True)
    gate_part = jnp.einsum(
        "scd,df->scf", received, gate_weight[0], preferred_element_type=jnp.float32
    )
    up_part = jnp.einsum("scd,df->scf", received, up_weight[0], preferred_element_type=jnp.float32)
    inner = (jax.nn.relu(gate_part) * up_part).astype(jnp.bfloat16)
    processed = jnp.einsum(
        "scf,fd->scd", inner, down_weight[0], preferred_element_type=jnp.float32
    ).astype(jnp.bfloat16)
    returned = lax.all_to_all(processed, "expert", split_axis=0, concat_axis=0, tiled=True)
    returned_flat = returned.reshape(slot_total, returned.shape[2])
    route_out = jnp.dot(route_slots, returned_flat, preferred_element_type=jnp.float32).astype(
        jnp.bfloat16
    )
    route_out = route_out.reshape(token_count, route_count, -1)
    mixture = jnp.sum(gates[:, :, None] * route_out.astype(jnp.float32), axis=1)
    layer_out = (hidden + mixture).astype(jnp.bfloat16)
    last_len = decode_len[0, DEC_DEV - 1]
    moved_keys = lax.dynamic_update_slice(
        take_keys,
        fresh_keys[DEC_DEV - 1][None, None],
        (jnp.zeros((), jnp.int32), last_len, jnp.zeros((), jnp.int32)),
    )
    moved_values = lax.dynamic_update_slice(
        take_values,
        fresh_values[DEC_DEV - 1][None, None],
        (jnp.zeros((), jnp.int32), last_len, jnp.zeros((), jnp.int32)),
    )
    return (layer_out, moved_keys, moved_values)


def solution(mesh):
    return jax.shard_map(
        on_device,
        mesh=mesh,
        in_specs=(
            P(("dp", "expert"), None),
            P(("dp", "expert"), None),
            P(("dp", "expert"), None),
            P(("dp", "expert"), None),
            P(),
            P(),
            P(),
            P("expert", None, None),
            P("expert", None, None),
            P("expert", None, None),
            P(("dp", "expert"), None),
            P(("dp", "expert"), None, None),
            P(("dp", "expert"), None, None),
            P(("dp", "expert"), None),
            P(("dp", "expert"), None),
            P(("dp", "expert"), None),
            P(("dp", "expert")),
            P(("dp", "expert"), None, None),
            P(("dp", "expert"), None, None),
            P("expert", None),
        ),
        out_specs=(
            P(("dp", "expert"), None),
            P(("dp", "expert"), None, None),
            P(("dp", "expert"), None, None),
        ),
        check_vma=False,
    )
```

```python
import jax
import jax.numpy as jnp
from jax import lax
from jax.sharding import PartitionSpec as P

QUERY_HEADS = 12
KEY_VALUE_HEADS = 2
HEAD_SIZE = 128
DEC_DEV = 8
PCH = 128
CONTEXT_LENGTH = 512


def attend(query_row_block, key_row_block, value_row_block, valid):
    batch_groups = query_row_block.shape[0]
    query_total = query_row_block.shape[1]
    key_total = key_row_block.shape[1]
    grouped_rows = query_row_block.reshape(
        batch_groups, query_total, KEY_VALUE_HEADS, QUERY_HEADS // KEY_VALUE_HEADS, HEAD_SIZE
    )
    key_head_rows = key_row_block.reshape(batch_groups, key_total, KEY_VALUE_HEADS, HEAD_SIZE)
    value_head_rows = value_row_block.reshape(batch_groups, key_total, KEY_VALUE_HEADS, HEAD_SIZE)
    scores = jnp.einsum(
        "bqhgd,bkhd->bqhgk", grouped_rows, key_head_rows, preferred_element_type=jnp.float32
    ) * HEAD_SIZE ** (-0.5)
    weights = jnp.where(valid[:, :, None, None, :], jnp.exp(scores), 0.0)
    totals = jnp.sum(weights, axis=-1)
    mixed = (
        jnp.einsum(
            "bqhgk,bkhd->bqhgd",
            weights.astype(jnp.bfloat16),
            value_head_rows,
            preferred_element_type=jnp.float32,
        )
        / totals[..., None]
    )
    return mixed.reshape(batch_groups, query_total, QUERY_HEADS * HEAD_SIZE).astype(jnp.bfloat16)


def capacity_for(token_count, route_count, expert_count):
    return min(token_count, (token_count * route_count // expert_count * 3 // 2 + 7) // 8 * 8)


def page_lookup(table, pool_flat):
    pool_count = pool_flat.shape[0]
    selector = (table[..., None] == jnp.arange(pool_count, dtype=jnp.int32)).astype(jnp.bfloat16)
    return jnp.einsum(
        "...p,pk->...k", selector, pool_flat, preferred_element_type=jnp.float32
    ).astype(jnp.bfloat16)


def on_device(
    queries,
    fresh_keys,
    fresh_values,
    residual,
    norm_gain,
    out_weight,
    router_weight,
    gate_weight,
    up_weight,
    down_weight,
    expert_ids,
    paged_keys,
    paged_values,
    decode_table,
    prefill_table,
    decode_len,
    prefill_len,
    departing_keys,
    departing_values,
    destination,
):
    width_total = KEY_VALUE_HEADS * HEAD_SIZE
    target_row = destination[0]
    dp_count = target_row.shape[0]
    rows_total = departing_keys.shape[1]
    chunk_rows = rows_total // dp_count
    both = jnp.concatenate([departing_keys[0], departing_values[0]], axis=-1)
    both = both.reshape(dp_count, chunk_rows, 2 * width_total)
    spread = lax.all_to_all(both, "dp", split_axis=0, concat_axis=0, tiled=True)
    sources = jnp.sum(
        jnp.where(
            target_row[None, :] == jnp.arange(dp_count, dtype=jnp.int32)[:, None],
            jnp.arange(dp_count, dtype=jnp.int32)[None, :],
            0,
        ),
        axis=1,
    )
    routed = jnp.take(spread, sources, axis=0)
    gathered = lax.all_to_all(routed, "dp", split_axis=0, concat_axis=0, tiled=True)
    gathered = gathered.reshape(rows_total, 2 * width_total)
    take_keys = gathered[None, :, :width_total]
    take_values = gathered[None, :, width_total:]
    scale = HEAD_SIZE ** (-0.5)
    group = QUERY_HEADS // KEY_VALUE_HEADS
    token_count = queries.shape[0]
    resident_keys = jnp.take(paged_keys, decode_table.reshape(-1), axis=0).reshape(
        DEC_DEV - 1, CONTEXT_LENGTH, width_total
    )
    resident_values = jnp.take(paged_values, decode_table.reshape(-1), axis=0).reshape(
        DEC_DEV - 1, CONTEXT_LENGTH, width_total
    )
    context_keys = jnp.take(paged_keys, prefill_table[0], axis=0).reshape(
        CONTEXT_LENGTH, width_total
    )
    context_values = jnp.take(paged_values, prefill_table[0], axis=0).reshape(
        CONTEXT_LENGTH, width_total
    )
    positions = jnp.arange(CONTEXT_LENGTH, dtype=jnp.int32)
    decode_valid = (positions[None, :] < decode_len[0][:, None])[:, None, :]
    context_valid = (positions[None, :] < prefill_len[0])[:, None, :]
    block_pos = jnp.arange(PCH, dtype=jnp.int32)
    causal = (block_pos[None, :] <= block_pos[:, None])[:, None, :]
    query_heads = queries.reshape(token_count, QUERY_HEADS, HEAD_SIZE)
    per_group = []
    for g in range(KEY_VALUE_HEADS):
        lanes = slice(g * HEAD_SIZE, (g + 1) * HEAD_SIZE)
        q_g = query_heads[:, g * group : (g + 1) * group, :]
        q_dec = q_g[:DEC_DEV]
        q_pre = q_g[DEC_DEV:]
        f32 = jnp.float32
        s_res = jnp.einsum(
            "bjd,bkd->bjk", q_dec[: DEC_DEV - 1], resident_keys[..., lanes], preferred_element_type=f32
        )
        s_arr = jnp.einsum(
            "jd,kd->jk", q_dec[DEC_DEV - 1], take_keys[0, :, lanes], preferred_element_type=f32
        )
        s_cache = jnp.concatenate([s_res, s_arr[None]], axis=0) * scale
        s_new = jnp.einsum(
            "bjd,bd->bj", q_dec, fresh_keys[:DEC_DEV, lanes], preferred_element_type=f32
        ) * scale
        w_cache = jnp.where(decode_valid, jnp.exp(s_cache), 0.0)
        w_new = jnp.exp(s_new)
        total_dec = jnp.sum(w_cache, axis=-1) + w_new
        r_cache = w_cache.astype(jnp.bfloat16)
        r_new = w_new.astype(jnp.bfloat16).astype(f32)
        o_res = jnp.einsum(
            "bjk,bkd->bjd", r_cache[: DEC_DEV - 1], resident_values[..., lanes], preferred_element_type=f32
        )
        o_arr = jnp.einsum(
            "jk,kd->jd", r_cache[DEC_DEV - 1], take_values[0, :, lanes], preferred_element_type=f32
        )
        o_dec = jnp.concatenate([o_res, o_arr[None]], axis=0)
        o_dec = o_dec + r_new[..., None] * fresh_values[:DEC_DEV, None, lanes].astype(f32)
        o_dec = o_dec / total_dec[..., None]
        s_ctx = jnp.einsum(
            "tjd,kd->tjk", q_pre, context_keys[:, lanes], preferred_element_type=f32
        ) * scale
        s_blk = jnp.einsum(
            "tjd,kd->tjk", q_pre, fresh_keys[DEC_DEV:, lanes], preferred_element_type=f32
        ) * scale
        w_ctx = jnp.where(context_valid, jnp.exp(s_ctx), 0.0)
        w_blk = jnp.where(causal, jnp.exp(s_blk), 0.0)
        total_pre = jnp.sum(w_ctx, axis=-1) + jnp.sum(w_blk, axis=-1)
        o_pre = jnp.einsum(
            "tjk,kd->tjd", w_ctx.astype(jnp.bfloat16), context_values[:, lanes], preferred_element_type=f32
        ) + jnp.einsum(
            "tjk,kd->tjd", w_blk.astype(jnp.bfloat16), fresh_values[DEC_DEV:, lanes], preferred_element_type=f32
        )
        o_pre = o_pre / total_pre[..., None]
        per_group.append(jnp.concatenate([o_dec, o_pre], axis=0))
    attended = jnp.concatenate(per_group, axis=1).astype(jnp.bfloat16).reshape(
        token_count, QUERY_HEADS * HEAD_SIZE
    )
    hidden = residual.astype(jnp.float32) + jnp.dot(
        attended, out_weight, preferred_element_type=jnp.float32
    )
    variance = jnp.mean(hidden * hidden, axis=-1, keepdims=True)
    normed = (hidden * lax.rsqrt(variance + 1e-06) * norm_gain).astype(jnp.bfloat16)
    logits = jnp.dot(normed, router_weight, preferred_element_type=jnp.float32)
    expert_count = router_weight.shape[1]
    expert_range = jnp.arange(expert_count, dtype=jnp.int32)
    chosen = jnp.sum(
        jnp.where(expert_ids[:, :, None] == expert_range, logits[:, None, :], 0.0), axis=-1
    )
    chosen = jax.nn.sigmoid(chosen)
    gates = chosen / jnp.sum(chosen, axis=1, keepdims=True)
    route_count = expert_ids.shape[1]
    capacity = capacity_for(token_count, route_count, expert_count)
    slot_total = expert_count * capacity
    flat_ids = expert_ids.T.reshape(-1)
    hits = (flat_ids[:, None] == expert_range[None, :]).astype(jnp.int32)
    ranks = jnp.sum((jnp.cumsum(hits, axis=0) - 1) * hits, axis=1)
    slot_of_route = flat_ids * capacity + ranks
    route_slots = (
        slot_of_route[:, None] == jnp.arange(slot_total, dtype=jnp.int32)[None, :]
    ).astype(jnp.bfloat16)
    token_slots = jnp.sum(route_slots.reshape(route_count, token_count, slot_total), axis=0)
    outgoing = jnp.einsum(
        "ts,td->sd", token_slots, normed, preferred_element_type=jnp.float32
    ).astype(jnp.bfloat16)
    outgoing = outgoing.reshape(expert_count, capacity, normed.shape[1])
    received = lax.all_to_all(outgoing, "expert", split_axis=0, concat_axis=0, tiled=True)
    gate_part = jnp.einsum(
        "scd,df->scf", received, gate_weight[0], preferred_element_type=jnp.float32
    )
    up_part = jnp.einsum("scd,df->scf", received, up_weight[0], preferred_element_type=jnp.float32)
    inner = (jax.nn.relu(gate_part) * up_part).astype(jnp.bfloat16)
    processed = jnp.einsum(
        "scf,fd->scd", inner, down_weight[0], preferred_element_type=jnp.float32
    ).astype(jnp.bfloat16)
    returned = lax.all_to_all(processed, "expert", split_axis=0, concat_axis=0, tiled=True)
    returned_flat = returned.reshape(slot_total, returned.shape[2])
    route_out = jnp.take(returned_flat, slot_of_route, axis=0).reshape(
        route_count, token_count, -1
    )
    mixture = jnp.sum(gates.T[:, :, None] * route_out.astype(jnp.float32), axis=0)
    layer_out = (hidden + mixture).astype(jnp.bfloat16)
    last_len = decode_len[0, DEC_DEV - 1]
    moved_keys = lax.dynamic_update_slice(
        take_keys,
        fresh_keys[DEC_DEV - 1][None, None],
        (jnp.zeros((), jnp.int32), last_len, jnp.zeros((), jnp.int32)),
    )
    moved_values = lax.dynamic_update_slice(
        take_values,
        fresh_values[DEC_DEV - 1][None, None],
        (jnp.zeros((), jnp.int32), last_len, jnp.zeros((), jnp.int32)),
    )
    return (layer_out, moved_keys, moved_values)


def solution(mesh):
    return jax.shard_map(
        on_device,
        mesh=mesh,
        in_specs=(
            P(("dp", "expert"), None),
            P(("dp", "expert"), None),
            P(("dp", "expert"), None),
            P(("dp", "expert"), None),
            P(),
            P(),
            P(),
            P("expert", None, None),
            P("expert", None, None),
            P("expert", None, None),
            P(("dp", "expert"), None),
            P(("dp", "expert"), None, None),
            P(("dp", "expert"), None, None),
            P(("dp", "expert"), None),
            P(("dp", "expert"), None),
            P(("dp", "expert"), None),
            P(("dp", "expert")),
            P(("dp", "expert"), None, None),
            P(("dp", "expert"), None, None),
            P("expert", None),
        ),
        out_specs=(
            P(("dp", "expert"), None),
            P(("dp", "expert"), None, None),
            P(("dp", "expert"), None, None),
        ),
        check_vma=False,
    )
```

```python
import jax
import jax.numpy as jnp
from jax import lax
from jax.experimental import pallas as pl
from jax.experimental.pallas import tpu as pltpu
from jax.sharding import PartitionSpec as P

QUERY_HEADS = 12
KEY_VALUE_HEADS = 2
HEAD_SIZE = 128
DEC_DEV = 8
PCH = 128
CONTEXT_LENGTH = 512


def attention_kernel(dt_ref, pt_ref, dl_ref, plen_ref, q_ref, fk_ref, fv_ref, pk_ref, pv_ref, arrived_ref, o_ref):
    f32 = jnp.float32
    bf16 = jnp.bfloat16
    group = QUERY_HEADS // KEY_VALUE_HEADS
    scale = HEAD_SIZE ** (-0.5)
    page_rows = pk_ref.shape[1]
    pages = CONTEXT_LENGTH // page_rows
    nt = (((1,), (1,)), ((), ()))
    lane_pos = lax.broadcasted_iota(jnp.int32, (1, page_rows), 1)
    dec_rows = [[None] * QUERY_HEADS for _ in range(DEC_DEV)]
    for g in range(KEY_VALUE_HEADS):
        lanes = pl.ds(g * HEAD_SIZE, HEAD_SIZE)
        for b in range(DEC_DEV):
            length = dl_ref[0, b]
            q = jnp.concatenate(
                [q_ref[pl.ds(b, 1), pl.ds((g * group + j) * HEAD_SIZE, HEAD_SIZE)] for j in range(group)],
                axis=0,
            )
            kf = fk_ref[pl.ds(b, 1), lanes].astype(f32)
            vf = fv_ref[pl.ds(b, 1), lanes].astype(f32)
            w_new = jnp.exp(jnp.sum(q.astype(f32) * kf, axis=-1, keepdims=True) * scale)
            total = w_new
            acc = w_new.astype(bf16).astype(f32) * vf
            for p in range(pages):
                if b < DEC_DEV - 1:
                    page = dt_ref[b, p]
                    k = pk_ref[page, :, lanes]
                    v = pv_ref[page, :, lanes]
                else:
                    k = arrived_ref[pl.ds(p * page_rows, page_rows), lanes]
                    v = arrived_ref[pl.ds(p * page_rows, page_rows), pl.ds(KEY_VALUE_HEADS * HEAD_SIZE + g * HEAD_SIZE, HEAD_SIZE)]
                s = lax.dot_general(q, k, nt, preferred_element_type=f32) * scale
                w = jnp.where(lane_pos + p * page_rows < length, jnp.exp(s), 0.0)
                total = total + jnp.sum(w, axis=-1, keepdims=True)
                acc = acc + jnp.dot(w.astype(bf16), v, preferred_element_type=f32)
            out = acc / total
            for j in range(group):
                dec_rows[b][g * group + j] = out[j : j + 1]
    prefill_length = plen_ref[0]
    rows = group * PCH
    row_pos = lax.broadcasted_iota(jnp.int32, (rows, page_rows), 0) % PCH
    col_pos = lax.broadcasted_iota(jnp.int32, (rows, page_rows), 1)
    causal = col_pos <= row_pos
    for g in range(KEY_VALUE_HEADS):
        lanes = pl.ds(g * HEAD_SIZE, HEAD_SIZE)
        q = jnp.concatenate(
            [q_ref[:, pl.ds((g * group + j) * HEAD_SIZE, HEAD_SIZE)].astype(f32)[DEC_DEV:] for j in range(group)],
            axis=0,
        ).astype(bf16)
        kb = fk_ref[:, lanes].astype(f32)[DEC_DEV:].astype(bf16)
        vb = fv_ref[:, lanes].astype(f32)[DEC_DEV:].astype(bf16)
        s = lax.dot_general(q, kb, nt, preferred_element_type=f32) * scale
        w = jnp.where(causal, jnp.exp(s), 0.0)
        total = jnp.sum(w, axis=-1, keepdims=True)
        acc = jnp.dot(w.astype(bf16), vb, preferred_element_type=f32)
        for p in range(pages):
            page = pt_ref[0, p]
            k = pk_ref[page, :, lanes]
            v = pv_ref[page, :, lanes]
            s = lax.dot_general(q, k, nt, preferred_element_type=f32) * scale
            w = jnp.where(col_pos + p * page_rows < prefill_length, jnp.exp(s), 0.0)
            total = total + jnp.sum(w, axis=-1, keepdims=True)
            acc = acc + jnp.dot(w.astype(bf16), v, preferred_element_type=f32)
        out = acc / total
        for j in range(group):
            h = g * group + j
            dec_col = jnp.concatenate([dec_rows[b][h] for b in range(DEC_DEV)], axis=0)
            o_ref[:, pl.ds(h * HEAD_SIZE, HEAD_SIZE)] = jnp.concatenate(
                [dec_col, out[j * PCH : (j + 1) * PCH]], axis=0
            ).astype(o_ref.dtype)


def paged_attention(decode_table, prefill_table, decode_len, prefill_len, queries, fresh_keys, fresh_values, paged_keys, paged_values, arrived):
    smem = pl.BlockSpec(memory_space=pltpu.SMEM)
    vmem = pl.BlockSpec(memory_space=pltpu.VMEM)
    return pl.pallas_call(
        attention_kernel,
        out_shape=jax.ShapeDtypeStruct(queries.shape, queries.dtype),
        in_specs=[smem] * 4 + [vmem] * 6,
        out_specs=vmem,
    )(decode_table, prefill_table, decode_len, prefill_len, queries, fresh_keys, fresh_values, paged_keys, paged_values, arrived)


def capacity_for(token_count, route_count, expert_count):
    return min(token_count, (token_count * route_count // expert_count * 3 // 2 + 7) // 8 * 8)


def page_lookup(table, pool_flat):
    pool_count = pool_flat.shape[0]
    selector = (table[..., None] == jnp.arange(pool_count, dtype=jnp.int32)).astype(jnp.bfloat16)
    return jnp.einsum(
        "...p,pk->...k", selector, pool_flat, preferred_element_type=jnp.float32
    ).astype(jnp.bfloat16)


def on_device(
    queries,
    fresh_keys,
    fresh_values,
    residual,
    norm_gain,
    out_weight,
    router_weight,
    gate_weight,
    up_weight,
    down_weight,
    expert_ids,
    paged_keys,
    paged_values,
    decode_table,
    prefill_table,
    decode_len,
    prefill_len,
    departing_keys,
    departing_values,
    destination,
):
    width_total = KEY_VALUE_HEADS * HEAD_SIZE
    target_row = destination[0]
    dp_count = target_row.shape[0]
    rows_total = departing_keys.shape[1]
    chunk_rows = rows_total // dp_count
    both = jnp.concatenate([departing_keys[0], departing_values[0]], axis=-1)
    both = both.reshape(dp_count, chunk_rows, 2 * width_total)
    spread = lax.all_to_all(both, "dp", split_axis=0, concat_axis=0, tiled=True)
    sources = jnp.sum(
        jnp.where(
            target_row[None, :] == jnp.arange(dp_count, dtype=jnp.int32)[:, None],
            jnp.arange(dp_count, dtype=jnp.int32)[None, :],
            0,
        ),
        axis=1,
    )
    routed = jnp.take(spread, sources, axis=0)
    gathered = lax.all_to_all(routed, "dp", split_axis=0, concat_axis=0, tiled=True)
    gathered = gathered.reshape(rows_total, 2 * width_total)
    take_keys = gathered[None, :, :width_total]
    take_values = gathered[None, :, width_total:]
    token_count = queries.shape[0]
    attended = paged_attention(
        decode_table,
        prefill_table,
        decode_len,
        prefill_len,
        queries,
        fresh_keys,
        fresh_values,
        paged_keys,
        paged_values,
        gathered,
    )
    hidden = residual.astype(jnp.float32) + jnp.dot(
        attended, out_weight, preferred_element_type=jnp.float32
    )
    variance = jnp.mean(hidden * hidden, axis=-1, keepdims=True)
    normed = (hidden * lax.rsqrt(variance + 1e-06) * norm_gain).astype(jnp.bfloat16)
    logits = jnp.dot(normed, router_weight, preferred_element_type=jnp.float32)
    expert_count = router_weight.shape[1]
    expert_range = jnp.arange(expert_count, dtype=jnp.int32)
    chosen = jnp.sum(
        jnp.where(expert_ids[:, :, None] == expert_range, logits[:, None, :], 0.0), axis=-1
    )
    chosen = jax.nn.sigmoid(chosen)
    gates = chosen / jnp.sum(chosen, axis=1, keepdims=True)
    route_count = expert_ids.shape[1]
    capacity = capacity_for(token_count, route_count, expert_count)
    slot_total = expert_count * capacity
    flat_ids = expert_ids.T.reshape(-1)
    hits = (flat_ids[:, None] == expert_range[None, :]).astype(jnp.int32)
    ranks = jnp.sum((jnp.cumsum(hits, axis=0) - 1) * hits, axis=1)
    slot_of_route = flat_ids * capacity + ranks
    route_slots = (
        slot_of_route[:, None] == jnp.arange(slot_total, dtype=jnp.int32)[None, :]
    ).astype(jnp.bfloat16)
    token_slots = jnp.sum(route_slots.reshape(route_count, token_count, slot_total), axis=0)
    outgoing = jnp.einsum(
        "ts,td->sd", token_slots, normed, preferred_element_type=jnp.float32
    ).astype(jnp.bfloat16)
    outgoing = outgoing.reshape(expert_count, capacity, normed.shape[1])
    received = lax.all_to_all(outgoing, "expert", split_axis=0, concat_axis=0, tiled=True)
    gate_part = jnp.einsum(
        "scd,df->scf", received, gate_weight[0], preferred_element_type=jnp.float32
    )
    up_part = jnp.einsum("scd,df->scf", received, up_weight[0], preferred_element_type=jnp.float32)
    inner = (jax.nn.relu(gate_part) * up_part).astype(jnp.bfloat16)
    processed = jnp.einsum(
        "scf,fd->scd", inner, down_weight[0], preferred_element_type=jnp.float32
    ).astype(jnp.bfloat16)
    returned = lax.all_to_all(processed, "expert", split_axis=0, concat_axis=0, tiled=True)
    returned_flat = returned.reshape(slot_total, returned.shape[2])
    route_out = jnp.take(returned_flat, slot_of_route, axis=0).reshape(
        route_count, token_count, -1
    )
    mixture = jnp.sum(gates.T[:, :, None] * route_out.astype(jnp.float32), axis=0)
    layer_out = (hidden + mixture).astype(jnp.bfloat16)
    last_len = decode_len[0, DEC_DEV - 1]
    moved_keys = lax.dynamic_update_slice(
        take_keys,
        fresh_keys[DEC_DEV - 1][None, None],
        (jnp.zeros((), jnp.int32), last_len, jnp.zeros((), jnp.int32)),
    )
    moved_values = lax.dynamic_update_slice(
        take_values,
        fresh_values[DEC_DEV - 1][None, None],
        (jnp.zeros((), jnp.int32), last_len, jnp.zeros((), jnp.int32)),
    )
    return (layer_out, moved_keys, moved_values)


def solution(mesh):
    return jax.shard_map(
        on_device,
        mesh=mesh,
        in_specs=(
            P(("dp", "expert"), None),
            P(("dp", "expert"), None),
            P(("dp", "expert"), None),
            P(("dp", "expert"), None),
            P(),
            P(),
            P(),
            P("expert", None, None),
            P("expert", None, None),
            P("expert", None, None),
            P(("dp", "expert"), None),
            P(("dp", "expert"), None, None),
            P(("dp", "expert"), None, None),
            P(("dp", "expert"), None),
            P(("dp", "expert"), None),
            P(("dp", "expert"), None),
            P(("dp", "expert")),
            P(("dp", "expert"), None, None),
            P(("dp", "expert"), None, None),
            P("expert", None),
        ),
        out_specs=(
            P(("dp", "expert"), None),
            P(("dp", "expert"), None, None),
            P(("dp", "expert"), None, None),
        ),
        check_vma=False,
    )
```

```python
import functools

import jax
import jax.numpy as jnp
from jax import lax
from jax.experimental import pallas as pl
from jax.experimental.pallas import tpu as pltpu
from jax.sharding import PartitionSpec as P

QUERY_HEADS = 12
KEY_VALUE_HEADS = 2
HEAD_SIZE = 128
DEC_DEV = 8
PCH = 128
CONTEXT_LENGTH = 512


def attention_kernel(arrived_only, dt_ref, pt_ref, dl_ref, plen_ref, q_ref, fk_ref, fv_ref, pk_ref, pv_ref, arrived_ref, o_ref):
    f32 = jnp.float32
    bf16 = jnp.bfloat16
    group = QUERY_HEADS // KEY_VALUE_HEADS
    scale = HEAD_SIZE ** (-0.5)
    page_rows = pk_ref.shape[1]
    pages = CONTEXT_LENGTH // page_rows
    nt = (((1,), (1,)), ((), ()))
    lane_pos = lax.broadcasted_iota(jnp.int32, (1, page_rows), 1)
    dec_rows = [[None] * QUERY_HEADS for _ in range(DEC_DEV)]
    requests = [DEC_DEV - 1] if arrived_only else list(range(DEC_DEV - 1))
    for g in range(KEY_VALUE_HEADS):
        lanes = pl.ds(g * HEAD_SIZE, HEAD_SIZE)
        for b in requests:
            length = dl_ref[0, b]
            q = jnp.concatenate(
                [q_ref[pl.ds(b, 1), pl.ds((g * group + j) * HEAD_SIZE, HEAD_SIZE)] for j in range(group)],
                axis=0,
            )
            kf = fk_ref[pl.ds(b, 1), lanes].astype(f32)
            vf = fv_ref[pl.ds(b, 1), lanes].astype(f32)
            w_new = jnp.exp(jnp.sum(q.astype(f32) * kf, axis=-1, keepdims=True) * scale)
            total = w_new
            acc = w_new.astype(bf16).astype(f32) * vf
            for p in range(pages):
                if b < DEC_DEV - 1:
                    page = dt_ref[b, p]
                    k = pk_ref[page, :, lanes]
                    v = pv_ref[page, :, lanes]
                else:
                    k = arrived_ref[pl.ds(p * page_rows, page_rows), lanes]
                    v = arrived_ref[pl.ds(p * page_rows, page_rows), pl.ds(KEY_VALUE_HEADS * HEAD_SIZE + g * HEAD_SIZE, HEAD_SIZE)]
                s = lax.dot_general(q, k, nt, preferred_element_type=f32) * scale
                w = jnp.where(lane_pos + p * page_rows < length, jnp.exp(s), 0.0)
                total = total + jnp.sum(w, axis=-1, keepdims=True)
                acc = acc + jnp.dot(w.astype(bf16), v, preferred_element_type=f32)
            out = acc / total
            for j in range(group):
                dec_rows[b][g * group + j] = out[j : j + 1]
    if arrived_only:
        for h in range(QUERY_HEADS):
            o_ref[:, pl.ds(h * HEAD_SIZE, HEAD_SIZE)] = dec_rows[DEC_DEV - 1][h].astype(o_ref.dtype)
        return
    dec_rows[DEC_DEV - 1] = [jnp.zeros((1, HEAD_SIZE), f32)] * QUERY_HEADS
    prefill_length = plen_ref[0]
    rows = group * PCH
    row_pos = lax.broadcasted_iota(jnp.int32, (rows, page_rows), 0) % PCH
    col_pos = lax.broadcasted_iota(jnp.int32, (rows, page_rows), 1)
    causal = col_pos <= row_pos
    for g in range(KEY_VALUE_HEADS):
        lanes = pl.ds(g * HEAD_SIZE, HEAD_SIZE)
        q = jnp.concatenate(
            [q_ref[:, pl.ds((g * group + j) * HEAD_SIZE, HEAD_SIZE)].astype(f32)[DEC_DEV:] for j in range(group)],
            axis=0,
        ).astype(bf16)
        kb = fk_ref[:, lanes].astype(f32)[DEC_DEV:].astype(bf16)
        vb = fv_ref[:, lanes].astype(f32)[DEC_DEV:].astype(bf16)
        s = lax.dot_general(q, kb, nt, preferred_element_type=f32) * scale
        w = jnp.where(causal, jnp.exp(s), 0.0)
        total = jnp.sum(w, axis=-1, keepdims=True)
        acc = jnp.dot(w.astype(bf16), vb, preferred_element_type=f32)
        for p in range(pages):
            page = pt_ref[0, p]
            k = pk_ref[page, :, lanes]
            v = pv_ref[page, :, lanes]
            s = lax.dot_general(q, k, nt, preferred_element_type=f32) * scale
            w = jnp.where(col_pos + p * page_rows < prefill_length, jnp.exp(s), 0.0)
            total = total + jnp.sum(w, axis=-1, keepdims=True)
            acc = acc + jnp.dot(w.astype(bf16), v, preferred_element_type=f32)
        out = acc / total
        for j in range(group):
            h = g * group + j
            dec_col = jnp.concatenate([dec_rows[b][h] for b in range(DEC_DEV)], axis=0)
            o_ref[:, pl.ds(h * HEAD_SIZE, HEAD_SIZE)] = jnp.concatenate(
                [dec_col, out[j * PCH : (j + 1) * PCH]], axis=0
            ).astype(o_ref.dtype)


def paged_attention(arrived_only, decode_table, prefill_table, decode_len, prefill_len, queries, fresh_keys, fresh_values, paged_keys, paged_values, arrived):
    smem = pl.BlockSpec(memory_space=pltpu.SMEM)
    vmem = pl.BlockSpec(memory_space=pltpu.VMEM)
    rows = 1 if arrived_only else queries.shape[0]
    return pl.pallas_call(
        functools.partial(attention_kernel, arrived_only),
        out_shape=jax.ShapeDtypeStruct((rows, queries.shape[1]), queries.dtype),
        in_specs=[smem] * 4 + [vmem] * 6,
        out_specs=vmem,
    )(decode_table, prefill_table, decode_len, prefill_len, queries, fresh_keys, fresh_values, paged_keys, paged_values, arrived)


def capacity_for(token_count, route_count, expert_count):
    return min(token_count, (token_count * route_count // expert_count * 3 // 2 + 7) // 8 * 8)


def page_lookup(table, pool_flat):
    pool_count = pool_flat.shape[0]
    selector = (table[..., None] == jnp.arange(pool_count, dtype=jnp.int32)).astype(jnp.bfloat16)
    return jnp.einsum(
        "...p,pk->...k", selector, pool_flat, preferred_element_type=jnp.float32
    ).astype(jnp.bfloat16)


def on_device(
    queries,
    fresh_keys,
    fresh_values,
    residual,
    norm_gain,
    out_weight,
    router_weight,
    gate_weight,
    up_weight,
    down_weight,
    expert_ids,
    paged_keys,
    paged_values,
    decode_table,
    prefill_table,
    decode_len,
    prefill_len,
    departing_keys,
    departing_values,
    destination,
):
    width_total = KEY_VALUE_HEADS * HEAD_SIZE
    target_row = destination[0]
    dp_count = target_row.shape[0]
    both = jnp.concatenate([departing_keys[0], departing_values[0]], axis=-1)
    my_row = lax.axis_index("dp")
    source = jnp.sum(jnp.where(target_row == my_row, jnp.arange(dp_count, dtype=jnp.int32), 0))
    everyone = lax.all_gather(both[None], "dp", axis=0, tiled=True)
    gathered = lax.dynamic_index_in_dim(everyone, source, axis=0, keepdims=False)
    take_keys = gathered[None, :, :width_total]
    take_values = gathered[None, :, width_total:]
    token_count = queries.shape[0]
    table_args = (decode_table, prefill_table, decode_len, prefill_len, queries, fresh_keys, fresh_values)
    attended = paged_attention(False, *table_args, paged_keys, paged_values, both)
    attended_last = paged_attention(True, *table_args, paged_keys, paged_values, gathered)
    hidden = residual.astype(jnp.float32) + jnp.dot(
        attended, out_weight, preferred_element_type=jnp.float32
    )
    variance = jnp.mean(hidden * hidden, axis=-1, keepdims=True)
    normed = (hidden * lax.rsqrt(variance + 1e-06) * norm_gain).astype(jnp.bfloat16)
    logits = jnp.dot(normed, router_weight, preferred_element_type=jnp.float32)
    expert_count = router_weight.shape[1]
    expert_range = jnp.arange(expert_count, dtype=jnp.int32)
    chosen = jnp.sum(
        jnp.where(expert_ids[:, :, None] == expert_range, logits[:, None, :], 0.0), axis=-1
    )
    chosen = jax.nn.sigmoid(chosen)
    gates = chosen / jnp.sum(chosen, axis=1, keepdims=True)
    route_count = expert_ids.shape[1]
    capacity = capacity_for(token_count, route_count, expert_count)
    slot_total = expert_count * capacity
    route_token = jnp.arange(route_count * token_count, dtype=jnp.int32) % token_count
    excluded = route_token == DEC_DEV - 1
    flat_ids = jnp.where(excluded, -1, expert_ids.T.reshape(-1))
    hits = (flat_ids[:, None] == expert_range[None, :]).astype(jnp.int32)
    ranks = jnp.sum((jnp.cumsum(hits, axis=0) - 1) * hits, axis=1)
    slot_of_route = jnp.where(excluded, 0, flat_ids * capacity + ranks)
    route_slots = (
        (slot_of_route[:, None] == jnp.arange(slot_total, dtype=jnp.int32)[None, :])
        & ~excluded[:, None]
    ).astype(jnp.bfloat16)
    token_slots = jnp.sum(route_slots.reshape(route_count, token_count, slot_total), axis=0)
    outgoing = jnp.einsum(
        "ts,td->sd", token_slots, normed, preferred_element_type=jnp.float32
    ).astype(jnp.bfloat16)
    outgoing = outgoing.reshape(expert_count, capacity, normed.shape[1])
    received = lax.all_to_all(outgoing, "expert", split_axis=0, concat_axis=0, tiled=True)
    gate_part = jnp.einsum(
        "scd,df->scf", received, gate_weight[0], preferred_element_type=jnp.float32
    )
    up_part = jnp.einsum("scd,df->scf", received, up_weight[0], preferred_element_type=jnp.float32)
    inner = (jax.nn.relu(gate_part) * up_part).astype(jnp.bfloat16)
    processed = jnp.einsum(
        "scf,fd->scd", inner, down_weight[0], preferred_element_type=jnp.float32
    ).astype(jnp.bfloat16)
    returned = lax.all_to_all(processed, "expert", split_axis=0, concat_axis=0, tiled=True)
    returned_flat = returned.reshape(slot_total, returned.shape[2])
    route_out = jnp.take(returned_flat, slot_of_route, axis=0).reshape(
        route_count, token_count, -1
    )
    mixture = jnp.sum(gates.T[:, :, None] * route_out.astype(jnp.float32), axis=0)
    layer_out = (hidden + mixture).astype(jnp.bfloat16)
    last = DEC_DEV - 1
    hidden_last = residual[last : last + 1].astype(jnp.float32) + jnp.dot(
        attended_last, out_weight, preferred_element_type=jnp.float32
    )
    variance_last = jnp.mean(hidden_last * hidden_last, axis=-1, keepdims=True)
    normed_last = (hidden_last * lax.rsqrt(variance_last + 1e-06) * norm_gain).astype(jnp.bfloat16)
    logits_last = jnp.dot(normed_last, router_weight, preferred_element_type=jnp.float32)
    ids_last = expert_ids[last : last + 1]
    picked = jnp.sum(
        jnp.where(ids_last[:, :, None] == expert_range, logits_last[:, None, :], 0.0), axis=-1
    )
    picked = jax.nn.sigmoid(picked)
    gates_last = picked / jnp.sum(picked, axis=1, keepdims=True)
    coef_last = jnp.sum(
        jnp.where(ids_last[:, :, None] == expert_range, gates_last[:, :, None], 0.0), axis=1
    )
    rows_all = lax.all_gather(normed_last, "expert", axis=0, tiled=True)
    coef_all = lax.all_gather(coef_last, "expert", axis=0, tiled=True)
    my_expert = lax.axis_index("expert")
    coef_mine = jnp.sum(jnp.where(expert_range[None, :] == my_expert, coef_all, 0.0), axis=1)
    gate_rows = jnp.dot(rows_all, gate_weight[0], preferred_element_type=jnp.float32)
    up_rows = jnp.dot(rows_all, up_weight[0], preferred_element_type=jnp.float32)
    inner_rows = (jax.nn.relu(gate_rows) * up_rows).astype(jnp.bfloat16)
    out_rows = jnp.dot(inner_rows, down_weight[0], preferred_element_type=jnp.float32).astype(
        jnp.bfloat16
    )
    share = coef_mine[:, None] * out_rows.astype(jnp.float32)
    mixture_last = lax.psum_scatter(share, "expert", scatter_dimension=0, tiled=True)
    out_last = (hidden_last + mixture_last).astype(jnp.bfloat16)
    layer_out = lax.dynamic_update_slice(layer_out, out_last, (last, 0))
    last_len = decode_len[0, DEC_DEV - 1]
    moved_keys = lax.dynamic_update_slice(
        take_keys,
        fresh_keys[DEC_DEV - 1][None, None],
        (jnp.zeros((), jnp.int32), last_len, jnp.zeros((), jnp.int32)),
    )
    moved_values = lax.dynamic_update_slice(
        take_values,
        fresh_values[DEC_DEV - 1][None, None],
        (jnp.zeros((), jnp.int32), last_len, jnp.zeros((), jnp.int32)),
    )
    return (layer_out, moved_keys, moved_values)


def solution(mesh):
    return jax.shard_map(
        on_device,
        mesh=mesh,
        in_specs=(
            P(("dp", "expert"), None),
            P(("dp", "expert"), None),
            P(("dp", "expert"), None),
            P(("dp", "expert"), None),
            P(),
            P(),
            P(),
            P("expert", None, None),
            P("expert", None, None),
            P("expert", None, None),
            P(("dp", "expert"), None),
            P(("dp", "expert"), None, None),
            P(("dp", "expert"), None, None),
            P(("dp", "expert"), None),
            P(("dp", "expert"), None),
            P(("dp", "expert"), None),
            P(("dp", "expert")),
            P(("dp", "expert"), None, None),
            P(("dp", "expert"), None, None),
            P("expert", None),
        ),
        out_specs=(
            P(("dp", "expert"), None),
            P(("dp", "expert"), None, None),
            P(("dp", "expert"), None, None),
        ),
        check_vma=False,
    )
```

```python
import functools

import jax
import jax.numpy as jnp
from jax import lax
from jax.experimental import pallas as pl
from jax.experimental.pallas import tpu as pltpu
from jax.sharding import PartitionSpec as P

QUERY_HEADS = 12
KEY_VALUE_HEADS = 2
HEAD_SIZE = 128
DEC_DEV = 8
PCH = 128
CONTEXT_LENGTH = 512


def attention_kernel(arrived_only, dt_ref, pt_ref, dl_ref, plen_ref, q_ref, fk_ref, fv_ref, pk_ref, pv_ref, arrived_ref, o_ref):
    f32 = jnp.float32
    bf16 = jnp.bfloat16
    group = QUERY_HEADS // KEY_VALUE_HEADS
    scale = HEAD_SIZE ** (-0.5)
    page_rows = pk_ref.shape[1]
    pages = CONTEXT_LENGTH // page_rows
    nt = (((1,), (1,)), ((), ()))
    lane_pos = lax.broadcasted_iota(jnp.int32, (1, page_rows), 1)
    dec_rows = [[None] * QUERY_HEADS for _ in range(DEC_DEV)]
    requests = [DEC_DEV - 1] if arrived_only else list(range(DEC_DEV - 1))
    for g in range(KEY_VALUE_HEADS):
        lanes = pl.ds(g * HEAD_SIZE, HEAD_SIZE)
        for b in requests:
            length = dl_ref[0, b]
            q = jnp.concatenate(
                [q_ref[pl.ds(b, 1), pl.ds((g * group + j) * HEAD_SIZE, HEAD_SIZE)] for j in range(group)],
                axis=0,
            )
            kf = fk_ref[pl.ds(b, 1), lanes].astype(f32)
            vf = fv_ref[pl.ds(b, 1), lanes].astype(f32)
            w_new = jnp.exp(jnp.sum(q.astype(f32) * kf, axis=-1, keepdims=True) * scale)
            total = w_new
            acc = w_new.astype(bf16).astype(f32) * vf
            for p in range(pages):
                if b < DEC_DEV - 1:
                    page = dt_ref[b, p]
                    k = pk_ref[page, :, lanes]
                    v = pv_ref[page, :, lanes]
                else:
                    k = arrived_ref[pl.ds(p * page_rows, page_rows), lanes]
                    v = arrived_ref[pl.ds(p * page_rows, page_rows), pl.ds(KEY_VALUE_HEADS * HEAD_SIZE + g * HEAD_SIZE, HEAD_SIZE)]
                s = lax.dot_general(q, k, nt, preferred_element_type=f32) * scale
                w = jnp.where(lane_pos + p * page_rows < length, jnp.exp(s), 0.0)
                total = total + jnp.sum(w, axis=-1, keepdims=True)
                acc = acc + jnp.dot(w.astype(bf16), v, preferred_element_type=f32)
            out = acc / total
            for j in range(group):
                dec_rows[b][g * group + j] = out[j : j + 1]
    if arrived_only:
        for h in range(QUERY_HEADS):
            o_ref[:, pl.ds(h * HEAD_SIZE, HEAD_SIZE)] = dec_rows[DEC_DEV - 1][h].astype(o_ref.dtype)
        return
    dec_rows[DEC_DEV - 1] = [jnp.zeros((1, HEAD_SIZE), f32)] * QUERY_HEADS
    prefill_length = plen_ref[0]
    rows = group * PCH
    row_pos = lax.broadcasted_iota(jnp.int32, (rows, page_rows), 0) % PCH
    col_pos = lax.broadcasted_iota(jnp.int32, (rows, page_rows), 1)
    causal = col_pos <= row_pos
    for g in range(KEY_VALUE_HEADS):
        lanes = pl.ds(g * HEAD_SIZE, HEAD_SIZE)
        q = jnp.concatenate(
            [q_ref[:, pl.ds((g * group + j) * HEAD_SIZE, HEAD_SIZE)].astype(f32)[DEC_DEV:] for j in range(group)],
            axis=0,
        ).astype(bf16)
        kb = fk_ref[:, lanes].astype(f32)[DEC_DEV:].astype(bf16)
        vb = fv_ref[:, lanes].astype(f32)[DEC_DEV:].astype(bf16)
        s = lax.dot_general(q, kb, nt, preferred_element_type=f32) * scale
        w = jnp.where(causal, jnp.exp(s), 0.0)
        total = jnp.sum(w, axis=-1, keepdims=True)
        acc = jnp.dot(w.astype(bf16), vb, preferred_element_type=f32)
        for p in range(pages):
            page = pt_ref[0, p]
            k = pk_ref[page, :, lanes]
            v = pv_ref[page, :, lanes]
            s = lax.dot_general(q, k, nt, preferred_element_type=f32) * scale
            w = jnp.where(col_pos + p * page_rows < prefill_length, jnp.exp(s), 0.0)
            total = total + jnp.sum(w, axis=-1, keepdims=True)
            acc = acc + jnp.dot(w.astype(bf16), v, preferred_element_type=f32)
        out = acc / total
        for j in range(group):
            h = g * group + j
            dec_col = jnp.concatenate([dec_rows[b][h] for b in range(DEC_DEV)], axis=0)
            o_ref[:, pl.ds(h * HEAD_SIZE, HEAD_SIZE)] = jnp.concatenate(
                [dec_col, out[j * PCH : (j + 1) * PCH]], axis=0
            ).astype(o_ref.dtype)


def paged_attention(arrived_only, decode_table, prefill_table, decode_len, prefill_len, queries, fresh_keys, fresh_values, paged_keys, paged_values, arrived):
    smem = pl.BlockSpec(memory_space=pltpu.SMEM)
    vmem = pl.BlockSpec(memory_space=pltpu.VMEM)
    rows = 1 if arrived_only else queries.shape[0]
    return pl.pallas_call(
        functools.partial(attention_kernel, arrived_only),
        out_shape=jax.ShapeDtypeStruct((rows, queries.shape[1]), queries.dtype),
        in_specs=[smem] * 4 + [vmem] * 6,
        out_specs=vmem,
    )(decode_table, prefill_table, decode_len, prefill_len, queries, fresh_keys, fresh_values, paged_keys, paged_values, arrived)


def capacity_for(token_count, route_count, expert_count):
    return min(token_count, (token_count * route_count // expert_count * 3 // 2 + 7) // 8 * 8)


def page_lookup(table, pool_flat):
    pool_count = pool_flat.shape[0]
    selector = (table[..., None] == jnp.arange(pool_count, dtype=jnp.int32)).astype(jnp.bfloat16)
    return jnp.einsum(
        "...p,pk->...k", selector, pool_flat, preferred_element_type=jnp.float32
    ).astype(jnp.bfloat16)


def on_device(
    queries,
    fresh_keys,
    fresh_values,
    residual,
    norm_gain,
    out_weight,
    router_weight,
    gate_weight,
    up_weight,
    down_weight,
    expert_ids,
    paged_keys,
    paged_values,
    decode_table,
    prefill_table,
    decode_len,
    prefill_len,
    departing_keys,
    departing_values,
    destination,
):
    width_total = KEY_VALUE_HEADS * HEAD_SIZE
    target_row = destination[0]
    dp_count = target_row.shape[0]
    both = jnp.concatenate([departing_keys[0], departing_values[0]], axis=-1)
    my_row = lax.axis_index("dp")
    source = jnp.sum(jnp.where(target_row == my_row, jnp.arange(dp_count, dtype=jnp.int32), 0))
    everyone = lax.all_gather(both[None], "dp", axis=0, tiled=True)
    gathered = lax.dynamic_index_in_dim(everyone, source, axis=0, keepdims=False)
    take_keys = gathered[None, :, :width_total]
    take_values = gathered[None, :, width_total:]
    token_count = queries.shape[0]
    table_args = (decode_table, prefill_table, decode_len, prefill_len, queries, fresh_keys, fresh_values)
    attended = paged_attention(False, *table_args, paged_keys, paged_values, both)
    attended_last = paged_attention(True, *table_args, paged_keys, paged_values, gathered)
    hidden = residual.astype(jnp.float32) + jnp.dot(
        attended, out_weight, preferred_element_type=jnp.float32
    )
    variance = jnp.mean(hidden * hidden, axis=-1, keepdims=True)
    normed = (hidden * lax.rsqrt(variance + 1e-06) * norm_gain).astype(jnp.bfloat16)
    logits = jnp.dot(normed, router_weight, preferred_element_type=jnp.float32)
    expert_count = router_weight.shape[1]
    expert_range = jnp.arange(expert_count, dtype=jnp.int32)
    chosen = jnp.sum(
        jnp.where(expert_ids[:, :, None] == expert_range, logits[:, None, :], 0.0), axis=-1
    )
    chosen = jax.nn.sigmoid(chosen)
    gates = chosen / jnp.sum(chosen, axis=1, keepdims=True)
    route_count = expert_ids.shape[1]
    capacity = capacity_for(token_count, route_count, expert_count)
    slot_total = expert_count * capacity
    route_token = jnp.arange(route_count * token_count, dtype=jnp.int32) % token_count
    excluded = route_token == DEC_DEV - 1
    flat_ids = jnp.where(excluded, -1, expert_ids.T.reshape(-1))
    hits = (flat_ids[:, None] == expert_range[None, :]).astype(jnp.int32)
    ranks = jnp.sum((jnp.cumsum(hits, axis=0) - 1) * hits, axis=1)
    slot_of_route = jnp.where(excluded, 0, flat_ids * capacity + ranks)
    route_slots = (
        (slot_of_route[:, None] == jnp.arange(slot_total, dtype=jnp.int32)[None, :])
        & ~excluded[:, None]
    ).astype(jnp.bfloat16)
    token_slots = jnp.sum(route_slots.reshape(route_count, token_count, slot_total), axis=0)
    outgoing = jnp.einsum(
        "ts,td->sd", token_slots, normed, preferred_element_type=jnp.float32
    ).astype(jnp.bfloat16)
    outgoing = outgoing.reshape(expert_count, capacity, normed.shape[1])
    received = lax.all_to_all(outgoing, "expert", split_axis=0, concat_axis=0, tiled=True)
    gate_part = jnp.einsum(
        "scd,df->scf", received, gate_weight[0], preferred_element_type=jnp.float32
    )
    up_part = jnp.einsum("scd,df->scf", received, up_weight[0], preferred_element_type=jnp.float32)
    inner = (jax.nn.relu(gate_part) * up_part).astype(jnp.bfloat16)
    processed = jnp.einsum(
        "scf,fd->scd", inner, down_weight[0], preferred_element_type=jnp.float32
    ).astype(jnp.bfloat16)
    returned = lax.all_to_all(processed, "expert", split_axis=0, concat_axis=0, tiled=True)
    returned_flat = returned.reshape(slot_total, returned.shape[2])
    route_out = jnp.take(returned_flat, slot_of_route, axis=0).reshape(
        route_count, token_count, -1
    )
    mixture = jnp.sum(gates.T[:, :, None] * route_out.astype(jnp.float32), axis=0)
    layer_out = (hidden + mixture).astype(jnp.bfloat16)
    last = DEC_DEV - 1
    hidden_last = residual[last : last + 1].astype(jnp.float32) + jnp.dot(
        attended_last, out_weight, preferred_element_type=jnp.float32
    )
    variance_last = jnp.mean(hidden_last * hidden_last, axis=-1, keepdims=True)
    normed_last = (hidden_last * lax.rsqrt(variance_last + 1e-06) * norm_gain).astype(jnp.bfloat16)
    logits_last = jnp.dot(normed_last, router_weight, preferred_element_type=jnp.float32)
    ids_last = expert_ids[last : last + 1]
    picked = jnp.sum(
        jnp.where(ids_last[:, :, None] == expert_range, logits_last[:, None, :], 0.0), axis=-1
    )
    picked = jax.nn.sigmoid(picked)
    gates_last = picked / jnp.sum(picked, axis=1, keepdims=True)
    coef_last = jnp.sum(
        jnp.where(ids_last[:, :, None] == expert_range, gates_last[:, :, None], 0.0), axis=1
    )
    sent_last = jnp.broadcast_to(normed_last[None], (expert_count, 1, normed_last.shape[1]))
    rows_all = lax.all_to_all(sent_last, "expert", split_axis=0, concat_axis=0, tiled=True)
    rows_all = rows_all.reshape(expert_count, normed_last.shape[1])
    gate_rows = jnp.dot(rows_all, gate_weight[0], preferred_element_type=jnp.float32)
    up_rows = jnp.dot(rows_all, up_weight[0], preferred_element_type=jnp.float32)
    inner_rows = (jax.nn.relu(gate_rows) * up_rows).astype(jnp.bfloat16)
    out_rows = jnp.dot(inner_rows, down_weight[0], preferred_element_type=jnp.float32).astype(
        jnp.bfloat16
    )
    back_last = lax.all_to_all(
        out_rows.reshape(expert_count, 1, -1), "expert", split_axis=0, concat_axis=0, tiled=True
    ).reshape(expert_count, -1)
    mixture_last = jnp.sum(coef_last.T * back_last.astype(jnp.float32), axis=0, keepdims=True)
    out_last = (hidden_last + mixture_last).astype(jnp.bfloat16)
    layer_out = lax.dynamic_update_slice(layer_out, out_last, (last, 0))
    last_len = decode_len[0, DEC_DEV - 1]
    moved_keys = lax.dynamic_update_slice(
        take_keys,
        fresh_keys[DEC_DEV - 1][None, None],
        (jnp.zeros((), jnp.int32), last_len, jnp.zeros((), jnp.int32)),
    )
    moved_values = lax.dynamic_update_slice(
        take_values,
        fresh_values[DEC_DEV - 1][None, None],
        (jnp.zeros((), jnp.int32), last_len, jnp.zeros((), jnp.int32)),
    )
    return (layer_out, moved_keys, moved_values)


def solution(mesh):
    return jax.shard_map(
        on_device,
        mesh=mesh,
        in_specs=(
            P(("dp", "expert"), None),
            P(("dp", "expert"), None),
            P(("dp", "expert"), None),
            P(("dp", "expert"), None),
            P(),
            P(),
            P(),
            P("expert", None, None),
            P("expert", None, None),
            P("expert", None, None),
            P(("dp", "expert"), None),
            P(("dp", "expert"), None, None),
            P(("dp", "expert"), None, None),
            P(("dp", "expert"), None),
            P(("dp", "expert"), None),
            P(("dp", "expert"), None),
            P(("dp", "expert")),
            P(("dp", "expert"), None, None),
            P(("dp", "expert"), None, None),
            P("expert", None),
        ),
        out_specs=(
            P(("dp", "expert"), None),
            P(("dp", "expert"), None, None),
            P(("dp", "expert"), None, None),
        ),
        check_vma=False,
    )
```

```python
import functools

import jax
import jax.numpy as jnp
from jax import lax
from jax.experimental import pallas as pl
from jax.experimental.pallas import tpu as pltpu
from jax.sharding import PartitionSpec as P

QUERY_HEADS = 12
KEY_VALUE_HEADS = 2
HEAD_SIZE = 128
DEC_DEV = 8
PCH = 128
CONTEXT_LENGTH = 512


def attention_kernel(arrived_only, dt_ref, pt_ref, dl_ref, plen_ref, q_ref, fk_ref, fv_ref, pk_ref, pv_ref, arrived_ref, o_ref):
    f32 = jnp.float32
    bf16 = jnp.bfloat16
    group = QUERY_HEADS // KEY_VALUE_HEADS
    scale = HEAD_SIZE ** (-0.5)
    page_rows = pk_ref.shape[1]
    pages = CONTEXT_LENGTH // page_rows
    nt = (((1,), (1,)), ((), ()))
    lane_pos = lax.broadcasted_iota(jnp.int32, (1, page_rows), 1)
    dec_rows = [[None] * QUERY_HEADS for _ in range(DEC_DEV)]
    requests = [DEC_DEV - 1] if arrived_only else list(range(DEC_DEV - 1))
    for g in range(KEY_VALUE_HEADS):
        lanes = pl.ds(g * HEAD_SIZE, HEAD_SIZE)
        for b in requests:
            length = dl_ref[0, b]
            q = jnp.concatenate(
                [q_ref[pl.ds(b, 1), pl.ds((g * group + j) * HEAD_SIZE, HEAD_SIZE)] for j in range(group)],
                axis=0,
            )
            kf = fk_ref[pl.ds(b, 1), lanes].astype(f32)
            vf = fv_ref[pl.ds(b, 1), lanes].astype(f32)
            w_new = jnp.exp(jnp.sum(q.astype(f32) * kf, axis=-1, keepdims=True) * scale)
            total = w_new
            acc = w_new.astype(bf16).astype(f32) * vf
            for p in range(pages):
                if b < DEC_DEV - 1:
                    page = dt_ref[b, p]
                    k = pk_ref[page, :, lanes]
                    v = pv_ref[page, :, lanes]
                else:
                    k = arrived_ref[pl.ds(p * page_rows, page_rows), lanes]
                    v = arrived_ref[pl.ds(p * page_rows, page_rows), pl.ds(KEY_VALUE_HEADS * HEAD_SIZE + g * HEAD_SIZE, HEAD_SIZE)]
                s = lax.dot_general(q, k, nt, preferred_element_type=f32) * scale
                w = jnp.where(lane_pos + p * page_rows < length, jnp.exp(s), 0.0)
                total = total + jnp.sum(w, axis=-1, keepdims=True)
                acc = acc + jnp.dot(w.astype(bf16), v, preferred_element_type=f32)
            out = acc / total
            for j in range(group):
                dec_rows[b][g * group + j] = out[j : j + 1]
    if arrived_only:
        for h in range(QUERY_HEADS):
            o_ref[:, pl.ds(h * HEAD_SIZE, HEAD_SIZE)] = dec_rows[DEC_DEV - 1][h].astype(o_ref.dtype)
        return
    dec_rows[DEC_DEV - 1] = [jnp.zeros((1, HEAD_SIZE), f32)] * QUERY_HEADS
    prefill_length = plen_ref[0]
    rows = group * PCH
    row_pos = lax.broadcasted_iota(jnp.int32, (rows, page_rows), 0) % PCH
    col_pos = lax.broadcasted_iota(jnp.int32, (rows, page_rows), 1)
    causal = col_pos <= row_pos
    for g in range(KEY_VALUE_HEADS):
        lanes = pl.ds(g * HEAD_SIZE, HEAD_SIZE)
        q = jnp.concatenate(
            [q_ref[:, pl.ds((g * group + j) * HEAD_SIZE, HEAD_SIZE)].astype(f32)[DEC_DEV:] for j in range(group)],
            axis=0,
        ).astype(bf16)
        kb = fk_ref[:, lanes].astype(f32)[DEC_DEV:].astype(bf16)
        vb = fv_ref[:, lanes].astype(f32)[DEC_DEV:].astype(bf16)
        s = lax.dot_general(q, kb, nt, preferred_element_type=f32) * scale
        w = jnp.where(causal, jnp.exp(s), 0.0)
        total = jnp.sum(w, axis=-1, keepdims=True)
        acc = jnp.dot(w.astype(bf16), vb, preferred_element_type=f32)
        for p in range(pages):
            page = pt_ref[0, p]
            k = pk_ref[page, :, lanes]
            v = pv_ref[page, :, lanes]
            s = lax.dot_general(q, k, nt, preferred_element_type=f32) * scale
            w = jnp.where(col_pos + p * page_rows < prefill_length, jnp.exp(s), 0.0)
            total = total + jnp.sum(w, axis=-1, keepdims=True)
            acc = acc + jnp.dot(w.astype(bf16), v, preferred_element_type=f32)
        out = acc / total
        for j in range(group):
            h = g * group + j
            dec_col = jnp.concatenate([dec_rows[b][h] for b in range(DEC_DEV)], axis=0)
            o_ref[:, pl.ds(h * HEAD_SIZE, HEAD_SIZE)] = jnp.concatenate(
                [dec_col, out[j * PCH : (j + 1) * PCH]], axis=0
            ).astype(o_ref.dtype)


def paged_attention(arrived_only, decode_table, prefill_table, decode_len, prefill_len, queries, fresh_keys, fresh_values, paged_keys, paged_values, arrived):
    smem = pl.BlockSpec(memory_space=pltpu.SMEM)
    vmem = pl.BlockSpec(memory_space=pltpu.VMEM)
    rows = 1 if arrived_only else queries.shape[0]
    return pl.pallas_call(
        functools.partial(attention_kernel, arrived_only),
        out_shape=jax.ShapeDtypeStruct((rows, queries.shape[1]), queries.dtype),
        in_specs=[smem] * 4 + [vmem] * 6,
        out_specs=vmem,
    )(decode_table, prefill_table, decode_len, prefill_len, queries, fresh_keys, fresh_values, paged_keys, paged_values, arrived)


def capacity_for(token_count, route_count, expert_count):
    return min(token_count, (token_count * route_count // expert_count * 3 // 2 + 7) // 8 * 8)


def page_lookup(table, pool_flat):
    pool_count = pool_flat.shape[0]
    selector = (table[..., None] == jnp.arange(pool_count, dtype=jnp.int32)).astype(jnp.bfloat16)
    return jnp.einsum(
        "...p,pk->...k", selector, pool_flat, preferred_element_type=jnp.float32
    ).astype(jnp.bfloat16)


def on_device(
    queries,
    fresh_keys,
    fresh_values,
    residual,
    norm_gain,
    out_weight,
    router_weight,
    gate_weight,
    up_weight,
    down_weight,
    expert_ids,
    paged_keys,
    paged_values,
    decode_table,
    prefill_table,
    decode_len,
    prefill_len,
    departing_keys,
    departing_values,
    destination,
):
    width_total = KEY_VALUE_HEADS * HEAD_SIZE
    target_row = destination[0]
    dp_count = target_row.shape[0]
    both = jnp.concatenate([departing_keys[0], departing_values[0]], axis=-1)
    my_row = lax.axis_index("dp")
    source = jnp.sum(jnp.where(target_row == my_row, jnp.arange(dp_count, dtype=jnp.int32), 0))
    everyone = lax.all_gather(both[None], "dp", axis=0, tiled=True)
    gathered = lax.dynamic_index_in_dim(everyone, source, axis=0, keepdims=False)
    take_keys = gathered[None, :, :width_total]
    take_values = gathered[None, :, width_total:]
    token_count = queries.shape[0]
    table_args = (decode_table, prefill_table, decode_len, prefill_len, queries, fresh_keys, fresh_values)
    attended = paged_attention(False, *table_args, paged_keys, paged_values, both)
    attended_last = paged_attention(True, *table_args, paged_keys, paged_values, gathered)
    hidden = residual.astype(jnp.float32) + jnp.dot(
        attended, out_weight, preferred_element_type=jnp.float32
    )
    variance = jnp.mean(hidden * hidden, axis=-1, keepdims=True)
    normed = (hidden * lax.rsqrt(variance + 1e-06) * norm_gain).astype(jnp.bfloat16)
    logits = jnp.dot(normed, router_weight, preferred_element_type=jnp.float32)
    expert_count = router_weight.shape[1]
    expert_range = jnp.arange(expert_count, dtype=jnp.int32)
    chosen = jnp.sum(
        jnp.where(expert_ids[:, :, None] == expert_range, logits[:, None, :], 0.0), axis=-1
    )
    chosen = jax.nn.sigmoid(chosen)
    gates = chosen / jnp.sum(chosen, axis=1, keepdims=True)
    route_count = expert_ids.shape[1]
    capacity = capacity_for(token_count, route_count, expert_count)
    slot_total = expert_count * capacity
    route_token = jnp.arange(route_count * token_count, dtype=jnp.int32) % token_count
    excluded = route_token == DEC_DEV - 1
    flat_ids = jnp.where(excluded, -1, expert_ids.T.reshape(-1))
    hits = (flat_ids[:, None] == expert_range[None, :]).astype(jnp.int32)
    ranks = jnp.sum((jnp.cumsum(hits, axis=0) - 1) * hits, axis=1)
    slot_of_route = jnp.where(excluded, 0, flat_ids * capacity + ranks)
    route_slots = (
        (slot_of_route[:, None] == jnp.arange(slot_total, dtype=jnp.int32)[None, :])
        & ~excluded[:, None]
    ).astype(jnp.bfloat16)
    token_slots = jnp.sum(route_slots.reshape(route_count, token_count, slot_total), axis=0)
    outgoing = jnp.einsum(
        "ts,td->sd", token_slots, normed, preferred_element_type=jnp.float32
    ).astype(jnp.bfloat16)
    outgoing = outgoing.reshape(expert_count, capacity, normed.shape[1])
    received = lax.all_to_all(outgoing, "expert", split_axis=0, concat_axis=0, tiled=True)
    gate_part = jnp.einsum(
        "scd,df->scf", received, gate_weight[0], preferred_element_type=jnp.float32
    )
    up_part = jnp.einsum("scd,df->scf", received, up_weight[0], preferred_element_type=jnp.float32)
    inner = (jax.nn.relu(gate_part) * up_part).astype(jnp.bfloat16)
    processed = jnp.einsum(
        "scf,fd->scd", inner, down_weight[0], preferred_element_type=jnp.float32
    ).astype(jnp.bfloat16)
    last = DEC_DEV - 1
    hidden_last = residual[last : last + 1].astype(jnp.float32) + jnp.dot(
        attended_last, out_weight, preferred_element_type=jnp.float32
    )
    variance_last = jnp.mean(hidden_last * hidden_last, axis=-1, keepdims=True)
    normed_last = (hidden_last * lax.rsqrt(variance_last + 1e-06) * norm_gain).astype(jnp.bfloat16)
    logits_last = jnp.dot(normed_last, router_weight, preferred_element_type=jnp.float32)
    ids_last = expert_ids[last : last + 1]
    picked = jnp.sum(
        jnp.where(ids_last[:, :, None] == expert_range, logits_last[:, None, :], 0.0), axis=-1
    )
    picked = jax.nn.sigmoid(picked)
    gates_last = picked / jnp.sum(picked, axis=1, keepdims=True)
    coef_last = jnp.sum(
        jnp.where(ids_last[:, :, None] == expert_range, gates_last[:, :, None], 0.0), axis=1
    )
    riders = jnp.broadcast_to(normed_last[None], (expert_count, 1, normed_last.shape[1]))
    outgoing_back = jnp.concatenate([processed, riders], axis=1)
    returned = lax.all_to_all(outgoing_back, "expert", split_axis=0, concat_axis=0, tiled=True)
    returned_flat = returned.reshape(expert_count * (capacity + 1), returned.shape[2])
    padded_slot = slot_of_route + slot_of_route // capacity
    route_out = jnp.take(returned_flat, padded_slot, axis=0).reshape(
        route_count, token_count, -1
    )
    rows_all = returned[:, capacity, :]
    mixture = jnp.sum(gates.T[:, :, None] * route_out.astype(jnp.float32), axis=0)
    layer_out = (hidden + mixture).astype(jnp.bfloat16)
    gate_rows = jnp.dot(rows_all, gate_weight[0], preferred_element_type=jnp.float32)
    up_rows = jnp.dot(rows_all, up_weight[0], preferred_element_type=jnp.float32)
    inner_rows = (jax.nn.relu(gate_rows) * up_rows).astype(jnp.bfloat16)
    out_rows = jnp.dot(inner_rows, down_weight[0], preferred_element_type=jnp.float32).astype(
        jnp.bfloat16
    )
    back_last = lax.all_to_all(
        out_rows.reshape(expert_count, 1, -1), "expert", split_axis=0, concat_axis=0, tiled=True
    ).reshape(expert_count, -1)
    mixture_last = jnp.sum(coef_last.T * back_last.astype(jnp.float32), axis=0, keepdims=True)
    out_last = (hidden_last + mixture_last).astype(jnp.bfloat16)
    layer_out = lax.dynamic_update_slice(layer_out, out_last, (last, 0))
    last_len = decode_len[0, DEC_DEV - 1]
    moved_keys = lax.dynamic_update_slice(
        take_keys,
        fresh_keys[DEC_DEV - 1][None, None],
        (jnp.zeros((), jnp.int32), last_len, jnp.zeros((), jnp.int32)),
    )
    moved_values = lax.dynamic_update_slice(
        take_values,
        fresh_values[DEC_DEV - 1][None, None],
        (jnp.zeros((), jnp.int32), last_len, jnp.zeros((), jnp.int32)),
    )
    return (layer_out, moved_keys, moved_values)


def solution(mesh):
    return jax.shard_map(
        on_device,
        mesh=mesh,
        in_specs=(
            P(("dp", "expert"), None),
            P(("dp", "expert"), None),
            P(("dp", "expert"), None),
            P(("dp", "expert"), None),
            P(),
            P(),
            P(),
            P("expert", None, None),
            P("expert", None, None),
            P("expert", None, None),
            P(("dp", "expert"), None),
            P(("dp", "expert"), None, None),
            P(("dp", "expert"), None, None),
            P(("dp", "expert"), None),
            P(("dp", "expert"), None),
            P(("dp", "expert"), None),
            P(("dp", "expert")),
            P(("dp", "expert"), None, None),
            P(("dp", "expert"), None, None),
            P("expert", None),
        ),
        out_specs=(
            P(("dp", "expert"), None),
            P(("dp", "expert"), None, None),
            P(("dp", "expert"), None, None),
        ),
        check_vma=False,
    )
```

```python
import functools

import jax
import jax.numpy as jnp
from jax import lax
from jax.experimental import pallas as pl
from jax.experimental.pallas import tpu as pltpu
from jax.sharding import PartitionSpec as P


QUERY_HEADS = 12
KEY_VALUE_HEADS = 2
HEAD_SIZE = 128
DEC_DEV = 8
PCH = 128
CONTEXT_LENGTH = 512


def attention_kernel(arrived_only, dt_ref, pt_ref, dl_ref, plen_ref, q_ref, fk_ref, fv_ref, pk_ref, pv_ref, arrived_ref, o_ref):
    f32 = jnp.float32
    bf16 = jnp.bfloat16
    group = QUERY_HEADS // KEY_VALUE_HEADS
    scale = HEAD_SIZE ** (-0.5)
    page_rows = pk_ref.shape[1]
    pages = CONTEXT_LENGTH // page_rows
    nt = (((1,), (1,)), ((), ()))
    lane_pos = lax.broadcasted_iota(jnp.int32, (1, page_rows), 1)
    dec_rows = [[None] * QUERY_HEADS for _ in range(DEC_DEV)]
    requests = [DEC_DEV - 1] if arrived_only else list(range(DEC_DEV - 1))
    for g in range(KEY_VALUE_HEADS):
        lanes = pl.ds(g * HEAD_SIZE, HEAD_SIZE)
        for b in requests:
            length = dl_ref[0, b]
            q = jnp.concatenate(
                [q_ref[pl.ds(b, 1), pl.ds((g * group + j) * HEAD_SIZE, HEAD_SIZE)] for j in range(group)],
                axis=0,
            )
            kf = fk_ref[pl.ds(b, 1), lanes].astype(f32)
            vf = fv_ref[pl.ds(b, 1), lanes].astype(f32)
            w_new = jnp.exp(jnp.sum(q.astype(f32) * kf, axis=-1, keepdims=True) * scale)
            total = w_new
            acc = w_new.astype(bf16).astype(f32) * vf
            for p in range(pages):
                if b < DEC_DEV - 1:
                    page = dt_ref[b, p]
                    k = pk_ref[page, :, lanes]
                    v = pv_ref[page, :, lanes]
                else:
                    k = arrived_ref[pl.ds(p * page_rows, page_rows), lanes]
                    v = arrived_ref[pl.ds(p * page_rows, page_rows), pl.ds(KEY_VALUE_HEADS * HEAD_SIZE + g * HEAD_SIZE, HEAD_SIZE)]
                s = lax.dot_general(q, k, nt, preferred_element_type=f32) * scale
                w = jnp.where(lane_pos + p * page_rows < length, jnp.exp(s), 0.0)
                total = total + jnp.sum(w, axis=-1, keepdims=True)
                acc = acc + jnp.dot(w.astype(bf16), v, preferred_element_type=f32)
            out = acc / total
            for j in range(group):
                dec_rows[b][g * group + j] = out[j : j + 1]
    if arrived_only:
        for h in range(QUERY_HEADS):
            o_ref[:, pl.ds(h * HEAD_SIZE, HEAD_SIZE)] = dec_rows[DEC_DEV - 1][h].astype(o_ref.dtype)
        return
    dec_rows[DEC_DEV - 1] = [jnp.zeros((1, HEAD_SIZE), f32)] * QUERY_HEADS
    prefill_length = plen_ref[0]
    rows = group * PCH
    row_pos = lax.broadcasted_iota(jnp.int32, (rows, page_rows), 0) % PCH
    col_pos = lax.broadcasted_iota(jnp.int32, (rows, page_rows), 1)
    causal = col_pos <= row_pos
    for g in range(KEY_VALUE_HEADS):
        lanes = pl.ds(g * HEAD_SIZE, HEAD_SIZE)
        q = jnp.concatenate(
            [q_ref[:, pl.ds((g * group + j) * HEAD_SIZE, HEAD_SIZE)].astype(f32)[DEC_DEV:] for j in range(group)],
            axis=0,
        ).astype(bf16)
        kb = fk_ref[:, lanes].astype(f32)[DEC_DEV:].astype(bf16)
        vb = fv_ref[:, lanes].astype(f32)[DEC_DEV:].astype(bf16)
        s = lax.dot_general(q, kb, nt, preferred_element_type=f32) * scale
        w = jnp.where(causal, jnp.exp(s), 0.0)
        total = jnp.sum(w, axis=-1, keepdims=True)
        acc = jnp.dot(w.astype(bf16), vb, preferred_element_type=f32)
        for p in range(pages):
            page = pt_ref[0, p]
            k = pk_ref[page, :, lanes]
            v = pv_ref[page, :, lanes]
            s = lax.dot_general(q, k, nt, preferred_element_type=f32) * scale
            w = jnp.where(col_pos + p * page_rows < prefill_length, jnp.exp(s), 0.0)
            total = total + jnp.sum(w, axis=-1, keepdims=True)
            acc = acc + jnp.dot(w.astype(bf16), v, preferred_element_type=f32)
        out = acc / total
        for j in range(group):
            h = g * group + j
            dec_col = jnp.concatenate([dec_rows[b][h] for b in range(DEC_DEV)], axis=0)
            o_ref[:, pl.ds(h * HEAD_SIZE, HEAD_SIZE)] = jnp.concatenate(
                [dec_col, out[j * PCH : (j + 1) * PCH]], axis=0
            ).astype(o_ref.dtype)


def paged_attention(arrived_only, decode_table, prefill_table, decode_len, prefill_len, queries, fresh_keys, fresh_values, paged_keys, paged_values, arrived):
    smem = pl.BlockSpec(memory_space=pltpu.SMEM)
    vmem = pl.BlockSpec(memory_space=pltpu.VMEM)
    rows = 1 if arrived_only else queries.shape[0]
    return pl.pallas_call(
        functools.partial(attention_kernel, arrived_only),
        out_shape=jax.ShapeDtypeStruct((rows, queries.shape[1]), queries.dtype),
        in_specs=[smem] * 4 + [vmem] * 6,
        out_specs=vmem,
    )(decode_table, prefill_table, decode_len, prefill_len, queries, fresh_keys, fresh_values, paged_keys, paged_values, arrived)


def capacity_for(token_count, route_count, expert_count):
    return min(token_count, (token_count * route_count // expert_count * 3 // 2 + 7) // 8 * 8)


def page_lookup(table, pool_flat):
    pool_count = pool_flat.shape[0]
    selector = (table[..., None] == jnp.arange(pool_count, dtype=jnp.int32)).astype(jnp.bfloat16)
    return jnp.einsum(
        "...p,pk->...k", selector, pool_flat, preferred_element_type=jnp.float32
    ).astype(jnp.bfloat16)


def on_device(
    queries,
    fresh_keys,
    fresh_values,
    residual,
    norm_gain,
    out_weight,
    router_weight,
    gate_weight,
    up_weight,
    down_weight,
    expert_ids,
    paged_keys,
    paged_values,
    decode_table,
    prefill_table,
    decode_len,
    prefill_len,
    departing_keys,
    departing_values,
    destination,
):
    width_total = KEY_VALUE_HEADS * HEAD_SIZE
    target_row = destination[0]
    dp_count = target_row.shape[0]
    both = jnp.concatenate([departing_keys[0], departing_values[0]], axis=-1)
    my_row = lax.axis_index("dp")
    shifts = jnp.arange(dp_count, dtype=jnp.int32)
    chunks = both.reshape(dp_count, -1, 2 * width_total)
    outward = jnp.take(chunks, (my_row + shifts) % dp_count, axis=0)
    held = [outward[0]]
    for s in range(1, dp_count):
        ring = [(i, (i + s) % dp_count) for i in range(dp_count)]
        held.append(lax.ppermute(outward[s], "dp", ring))
    held = jnp.stack(held)
    owner_of = jnp.sum(
        jnp.where(target_row[None, :] == shifts[:, None], shifts[None, :], 0), axis=1
    )
    wanted = owner_of[(my_row + shifts) % dp_count]
    forward = jnp.take(held, (my_row - wanted) % dp_count, axis=0)
    landed = [forward[0]]
    for s in range(1, dp_count):
        ring = [(i, (i + s) % dp_count) for i in range(dp_count)]
        landed.append(lax.ppermute(forward[s], "dp", ring))
    landed = jnp.stack(landed)
    gathered = jnp.take(landed, (my_row - shifts) % dp_count, axis=0).reshape(
        -1, 2 * width_total
    )
    take_keys = gathered[None, :, :width_total]
    take_values = gathered[None, :, width_total:]
    token_count = queries.shape[0]
    table_args = (decode_table, prefill_table, decode_len, prefill_len, queries, fresh_keys, fresh_values)
    attended = paged_attention(False, *table_args, paged_keys, paged_values, both)
    attended_last = paged_attention(True, *table_args, paged_keys, paged_values, gathered)
    hidden = residual.astype(jnp.float32) + jnp.dot(
        attended, out_weight, preferred_element_type=jnp.float32
    )
    variance = jnp.mean(hidden * hidden, axis=-1, keepdims=True)
    normed = (hidden * lax.rsqrt(variance + 1e-06) * norm_gain).astype(jnp.bfloat16)
    logits = jnp.dot(normed, router_weight, preferred_element_type=jnp.float32)
    expert_count = router_weight.shape[1]
    expert_range = jnp.arange(expert_count, dtype=jnp.int32)
    chosen = jnp.sum(
        jnp.where(expert_ids[:, :, None] == expert_range, logits[:, None, :], 0.0), axis=-1
    )
    chosen = jax.nn.sigmoid(chosen)
    gates = chosen / jnp.sum(chosen, axis=1, keepdims=True)
    route_count = expert_ids.shape[1]
    capacity = capacity_for(token_count, route_count, expert_count)
    slot_total = expert_count * capacity
    route_token = jnp.arange(route_count * token_count, dtype=jnp.int32) % token_count
    excluded = route_token == DEC_DEV - 1
    flat_ids = jnp.where(excluded, -1, expert_ids.T.reshape(-1))
    hits = (flat_ids[:, None] == expert_range[None, :]).astype(jnp.int32)
    ranks = jnp.sum((jnp.cumsum(hits, axis=0) - 1) * hits, axis=1)
    slot_of_route = jnp.where(excluded, 0, flat_ids * capacity + ranks)
    route_slots = (
        (slot_of_route[:, None] == jnp.arange(slot_total, dtype=jnp.int32)[None, :])
        & ~excluded[:, None]
    ).astype(jnp.bfloat16)
    token_slots = jnp.sum(route_slots.reshape(route_count, token_count, slot_total), axis=0)
    outgoing = jnp.einsum(
        "ts,td->sd", token_slots, normed, preferred_element_type=jnp.float32
    ).astype(jnp.bfloat16)
    outgoing = outgoing.reshape(expert_count, capacity, normed.shape[1])
    received = lax.all_to_all(outgoing, "expert", split_axis=0, concat_axis=0, tiled=True)
    gate_part = jnp.einsum(
        "scd,df->scf", received, gate_weight[0], preferred_element_type=jnp.float32
    )
    up_part = jnp.einsum("scd,df->scf", received, up_weight[0], preferred_element_type=jnp.float32)
    inner = (jax.nn.relu(gate_part) * up_part).astype(jnp.bfloat16)
    processed = jnp.einsum(
        "scf,fd->scd", inner, down_weight[0], preferred_element_type=jnp.float32
    ).astype(jnp.bfloat16)
    returned = lax.all_to_all(processed, "expert", split_axis=0, concat_axis=0, tiled=True)
    returned_flat = returned.reshape(slot_total, returned.shape[2])
    route_out = jnp.take(returned_flat, slot_of_route, axis=0).reshape(
        route_count, token_count, -1
    )
    mixture = jnp.sum(gates.T[:, :, None] * route_out.astype(jnp.float32), axis=0)
    layer_out = (hidden + mixture).astype(jnp.bfloat16)
    last = DEC_DEV - 1
    hidden_last = residual[last : last + 1].astype(jnp.float32) + jnp.dot(
        attended_last, out_weight, preferred_element_type=jnp.float32
    )
    variance_last = jnp.mean(hidden_last * hidden_last, axis=-1, keepdims=True)
    normed_last = (hidden_last * lax.rsqrt(variance_last + 1e-06) * norm_gain).astype(jnp.bfloat16)
    logits_last = jnp.dot(normed_last, router_weight, preferred_element_type=jnp.float32)
    ids_last = expert_ids[last : last + 1]
    picked = jnp.sum(
        jnp.where(ids_last[:, :, None] == expert_range, logits_last[:, None, :], 0.0), axis=-1
    )
    picked = jax.nn.sigmoid(picked)
    gates_last = picked / jnp.sum(picked, axis=1, keepdims=True)
    coef_last = jnp.sum(
        jnp.where(ids_last[:, :, None] == expert_range, gates_last[:, :, None], 0.0), axis=1
    )
    sent_last = jnp.broadcast_to(normed_last[None], (expert_count, 1, normed_last.shape[1]))
    rows_all = lax.all_to_all(sent_last, "expert", split_axis=0, concat_axis=0, tiled=True)
    rows_all = rows_all.reshape(expert_count, normed_last.shape[1])
    gate_rows = jnp.dot(rows_all, gate_weight[0], preferred_element_type=jnp.float32)
    up_rows = jnp.dot(rows_all, up_weight[0], preferred_element_type=jnp.float32)
    inner_rows = (jax.nn.relu(gate_rows) * up_rows).astype(jnp.bfloat16)
    out_rows = jnp.dot(inner_rows, down_weight[0], preferred_element_type=jnp.float32).astype(
        jnp.bfloat16
    )
    back_last = lax.all_to_all(
        out_rows.reshape(expert_count, 1, -1), "expert", split_axis=0, concat_axis=0, tiled=True
    ).reshape(expert_count, -1)
    mixture_last = jnp.sum(coef_last.T * back_last.astype(jnp.float32), axis=0, keepdims=True)
    out_last = (hidden_last + mixture_last).astype(jnp.bfloat16)
    layer_out = lax.dynamic_update_slice(layer_out, out_last, (last, 0))
    last_len = decode_len[0, DEC_DEV - 1]
    moved_keys = lax.dynamic_update_slice(
        take_keys,
        fresh_keys[DEC_DEV - 1][None, None],
        (jnp.zeros((), jnp.int32), last_len, jnp.zeros((), jnp.int32)),
    )
    moved_values = lax.dynamic_update_slice(
        take_values,
        fresh_values[DEC_DEV - 1][None, None],
        (jnp.zeros((), jnp.int32), last_len, jnp.zeros((), jnp.int32)),
    )
    return (layer_out, moved_keys, moved_values)


def solution(mesh):
    return jax.shard_map(
        on_device,
        mesh=mesh,
        in_specs=(
            P(("dp", "expert"), None),
            P(("dp", "expert"), None),
            P(("dp", "expert"), None),
            P(("dp", "expert"), None),
            P(),
            P(),
            P(),
            P("expert", None, None),
            P("expert", None, None),
            P("expert", None, None),
            P(("dp", "expert"), None),
            P(("dp", "expert"), None, None),
            P(("dp", "expert"), None, None),
            P(("dp", "expert"), None),
            P(("dp", "expert"), None),
            P(("dp", "expert"), None),
            P(("dp", "expert")),
            P(("dp", "expert"), None, None),
            P(("dp", "expert"), None, None),
            P("expert", None),
        ),
        out_specs=(
            P(("dp", "expert"), None),
            P(("dp", "expert"), None, None),
            P(("dp", "expert"), None, None),
        ),
        check_vma=False,
    )
```

```python
import functools

import jax
import jax.numpy as jnp
from jax import lax
from jax.experimental import pallas as pl
from jax.experimental.pallas import tpu as pltpu
from jax.sharding import PartitionSpec as P

QUERY_HEADS = 12
KEY_VALUE_HEADS = 2
HEAD_SIZE = 128
DEC_DEV = 8
PCH = 128
CONTEXT_LENGTH = 512


def attention_kernel(arrived_only, dt_ref, pt_ref, dl_ref, plen_ref, q_ref, fk_ref, fv_ref, pk_ref, pv_ref, arrived_ref, o_ref):
    f32 = jnp.float32
    bf16 = jnp.bfloat16
    group = QUERY_HEADS // KEY_VALUE_HEADS
    scale = HEAD_SIZE ** (-0.5)
    page_rows = pk_ref.shape[1]
    pages = CONTEXT_LENGTH // page_rows
    nt = (((1,), (1,)), ((), ()))
    lane_pos = lax.broadcasted_iota(jnp.int32, (1, page_rows), 1)
    dec_rows = [[None] * QUERY_HEADS for _ in range(DEC_DEV)]
    requests = [DEC_DEV - 1] if arrived_only else list(range(DEC_DEV - 1))
    for g in range(KEY_VALUE_HEADS):
        lanes = pl.ds(g * HEAD_SIZE, HEAD_SIZE)
        for b in requests:
            length = dl_ref[0, b]
            q = jnp.concatenate(
                [q_ref[pl.ds(b, 1), pl.ds((g * group + j) * HEAD_SIZE, HEAD_SIZE)] for j in range(group)],
                axis=0,
            )
            kf = fk_ref[pl.ds(b, 1), lanes].astype(f32)
            vf = fv_ref[pl.ds(b, 1), lanes].astype(f32)
            w_new = jnp.exp(jnp.sum(q.astype(f32) * kf, axis=-1, keepdims=True) * scale)
            total = w_new
            acc = w_new.astype(bf16).astype(f32) * vf
            for p in range(pages):
                if b < DEC_DEV - 1:
                    page = dt_ref[b, p]
                    k = pk_ref[page, :, lanes]
                    v = pv_ref[page, :, lanes]
                else:
                    k = arrived_ref[pl.ds(p * page_rows, page_rows), lanes]
                    v = arrived_ref[pl.ds(p * page_rows, page_rows), pl.ds(KEY_VALUE_HEADS * HEAD_SIZE + g * HEAD_SIZE, HEAD_SIZE)]
                s = lax.dot_general(q, k, nt, preferred_element_type=f32) * scale
                w = jnp.where(lane_pos + p * page_rows < length, jnp.exp(s), 0.0)
                total = total + jnp.sum(w, axis=-1, keepdims=True)
                acc = acc + jnp.dot(w.astype(bf16), v, preferred_element_type=f32)
            out = acc / total
            for j in range(group):
                dec_rows[b][g * group + j] = out[j : j + 1]
    if arrived_only:
        for h in range(QUERY_HEADS):
            o_ref[:, pl.ds(h * HEAD_SIZE, HEAD_SIZE)] = dec_rows[DEC_DEV - 1][h].astype(o_ref.dtype)
        return
    dec_rows[DEC_DEV - 1] = [jnp.zeros((1, HEAD_SIZE), f32)] * QUERY_HEADS
    prefill_length = plen_ref[0]
    rows = group * PCH
    row_pos = lax.broadcasted_iota(jnp.int32, (rows, page_rows), 0) % PCH
    col_pos = lax.broadcasted_iota(jnp.int32, (rows, page_rows), 1)
    causal = col_pos <= row_pos
    for g in range(KEY_VALUE_HEADS):
        lanes = pl.ds(g * HEAD_SIZE, HEAD_SIZE)
        q = jnp.concatenate(
            [q_ref[:, pl.ds((g * group + j) * HEAD_SIZE, HEAD_SIZE)].astype(f32)[DEC_DEV:] for j in range(group)],
            axis=0,
        ).astype(bf16)
        kb = fk_ref[:, lanes].astype(f32)[DEC_DEV:].astype(bf16)
        vb = fv_ref[:, lanes].astype(f32)[DEC_DEV:].astype(bf16)
        s = lax.dot_general(q, kb, nt, preferred_element_type=f32) * scale
        w = jnp.where(causal, jnp.exp(s), 0.0)
        total = jnp.sum(w, axis=-1, keepdims=True)
        acc = jnp.dot(w.astype(bf16), vb, preferred_element_type=f32)
        for p in range(pages):
            page = pt_ref[0, p]
            k = pk_ref[page, :, lanes]
            v = pv_ref[page, :, lanes]
            s = lax.dot_general(q, k, nt, preferred_element_type=f32) * scale
            w = jnp.where(col_pos + p * page_rows < prefill_length, jnp.exp(s), 0.0)
            total = total + jnp.sum(w, axis=-1, keepdims=True)
            acc = acc + jnp.dot(w.astype(bf16), v, preferred_element_type=f32)
        out = acc / total
        for j in range(group):
            h = g * group + j
            dec_col = jnp.concatenate([dec_rows[b][h] for b in range(DEC_DEV)], axis=0)
            o_ref[:, pl.ds(h * HEAD_SIZE, HEAD_SIZE)] = jnp.concatenate(
                [dec_col, out[j * PCH : (j + 1) * PCH]], axis=0
            ).astype(o_ref.dtype)


def paged_attention(arrived_only, decode_table, prefill_table, decode_len, prefill_len, queries, fresh_keys, fresh_values, paged_keys, paged_values, arrived):
    smem = pl.BlockSpec(memory_space=pltpu.SMEM)
    vmem = pl.BlockSpec(memory_space=pltpu.VMEM)
    rows = 1 if arrived_only else queries.shape[0]
    return pl.pallas_call(
        functools.partial(attention_kernel, arrived_only),
        out_shape=jax.ShapeDtypeStruct((rows, queries.shape[1]), queries.dtype),
        in_specs=[smem] * 4 + [vmem] * 6,
        out_specs=vmem,
    )(decode_table, prefill_table, decode_len, prefill_len, queries, fresh_keys, fresh_values, paged_keys, paged_values, arrived)


def capacity_for(token_count, route_count, expert_count):
    return min(token_count, (token_count * route_count // expert_count * 3 // 2 + 7) // 8 * 8)


def page_lookup(table, pool_flat):
    pool_count = pool_flat.shape[0]
    selector = (table[..., None] == jnp.arange(pool_count, dtype=jnp.int32)).astype(jnp.bfloat16)
    return jnp.einsum(
        "...p,pk->...k", selector, pool_flat, preferred_element_type=jnp.float32
    ).astype(jnp.bfloat16)


def on_device(
    queries,
    fresh_keys,
    fresh_values,
    residual,
    norm_gain,
    out_weight,
    router_weight,
    gate_weight,
    up_weight,
    down_weight,
    expert_ids,
    paged_keys,
    paged_values,
    decode_table,
    prefill_table,
    decode_len,
    prefill_len,
    departing_keys,
    departing_values,
    destination,
):
    width_total = KEY_VALUE_HEADS * HEAD_SIZE
    target_row = destination[0]
    dp_count = target_row.shape[0]
    rows_total = departing_keys.shape[1]
    chunk_rows = rows_total // dp_count
    both = jnp.concatenate([departing_keys[0], departing_values[0]], axis=-1)
    both = both.reshape(dp_count, chunk_rows, 2 * width_total)
    spread = lax.all_to_all(both, "dp", split_axis=0, concat_axis=0, tiled=True)
    sources = jnp.sum(
        jnp.where(
            target_row[None, :] == jnp.arange(dp_count, dtype=jnp.int32)[:, None],
            jnp.arange(dp_count, dtype=jnp.int32)[None, :],
            0,
        ),
        axis=1,
    )
    routed = jnp.take(spread, sources, axis=0)
    gathered = lax.all_to_all(routed, "dp", split_axis=0, concat_axis=0, tiled=True)
    gathered = gathered.reshape(rows_total, 2 * width_total)
    take_keys = gathered[None, :, :width_total]
    take_values = gathered[None, :, width_total:]
    token_count = queries.shape[0]
    table_args = (decode_table, prefill_table, decode_len, prefill_len, queries, fresh_keys, fresh_values)
    attended = paged_attention(False, *table_args, paged_keys, paged_values, both)
    attended_last = paged_attention(True, *table_args, paged_keys, paged_values, gathered)
    attended = lax.dynamic_update_slice(attended, attended_last, (DEC_DEV - 1, 0))
    hidden = residual.astype(jnp.float32) + jnp.dot(
        attended, out_weight, preferred_element_type=jnp.float32
    )
    variance = jnp.mean(hidden * hidden, axis=-1, keepdims=True)
    normed = (hidden * lax.rsqrt(variance + 1e-06) * norm_gain).astype(jnp.bfloat16)
    logits = jnp.dot(normed, router_weight, preferred_element_type=jnp.float32)
    expert_count = router_weight.shape[1]
    expert_range = jnp.arange(expert_count, dtype=jnp.int32)
    chosen = jnp.sum(
        jnp.where(expert_ids[:, :, None] == expert_range, logits[:, None, :], 0.0), axis=-1
    )
    chosen = jax.nn.sigmoid(chosen)
    gates = chosen / jnp.sum(chosen, axis=1, keepdims=True)
    route_count = expert_ids.shape[1]
    capacity = capacity_for(token_count, route_count, expert_count)
    slot_total = expert_count * capacity
    flat_ids = expert_ids.T.reshape(-1)
    hits = (flat_ids[:, None] == expert_range[None, :]).astype(jnp.int32)
    ranks = jnp.sum((jnp.cumsum(hits, axis=0) - 1) * hits, axis=1)
    slot_of_route = flat_ids * capacity + ranks
    route_slots = (
        slot_of_route[:, None] == jnp.arange(slot_total, dtype=jnp.int32)[None, :]
    ).astype(jnp.bfloat16)
    token_slots = jnp.sum(route_slots.reshape(route_count, token_count, slot_total), axis=0)
    outgoing = jnp.einsum(
        "ts,td->sd", token_slots, normed, preferred_element_type=jnp.float32
    ).astype(jnp.bfloat16)
    outgoing = outgoing.reshape(expert_count, capacity, normed.shape[1])
    received = lax.all_to_all(outgoing, "expert", split_axis=0, concat_axis=0, tiled=True)
    gate_part = jnp.einsum(
        "scd,df->scf", received, gate_weight[0], preferred_element_type=jnp.float32
    )
    up_part = jnp.einsum("scd,df->scf", received, up_weight[0], preferred_element_type=jnp.float32)
    inner = (jax.nn.relu(gate_part) * up_part).astype(jnp.bfloat16)
    processed = jnp.einsum(
        "scf,fd->scd", inner, down_weight[0], preferred_element_type=jnp.float32
    ).astype(jnp.bfloat16)
    returned = lax.all_to_all(processed, "expert", split_axis=0, concat_axis=0, tiled=True)
    returned_flat = returned.reshape(slot_total, returned.shape[2])
    route_out = jnp.dot(route_slots, returned_flat, preferred_element_type=jnp.float32).astype(
        jnp.bfloat16
    ).reshape(route_count, token_count, -1)
    mixture = jnp.sum(gates.T[:, :, None] * route_out.astype(jnp.float32), axis=0)
    layer_out = (hidden + mixture).astype(jnp.bfloat16)
    last_len = decode_len[0, DEC_DEV - 1]
    moved_keys = lax.dynamic_update_slice(
        take_keys,
        fresh_keys[DEC_DEV - 1][None, None],
        (jnp.zeros((), jnp.int32), last_len, jnp.zeros((), jnp.int32)),
    )
    moved_values = lax.dynamic_update_slice(
        take_values,
        fresh_values[DEC_DEV - 1][None, None],
        (jnp.zeros((), jnp.int32), last_len, jnp.zeros((), jnp.int32)),
    )
    return (layer_out, moved_keys, moved_values)


def solution(mesh):
    return jax.shard_map(
        on_device,
        mesh=mesh,
        in_specs=(
            P(("dp", "expert"), None),
            P(("dp", "expert"), None),
            P(("dp", "expert"), None),
            P(("dp", "expert"), None),
            P(),
            P(),
            P(),
            P("expert", None, None),
            P("expert", None, None),
            P("expert", None, None),
            P(("dp", "expert"), None),
            P(("dp", "expert"), None, None),
            P(("dp", "expert"), None, None),
            P(("dp", "expert"), None),
            P(("dp", "expert"), None),
            P(("dp", "expert"), None),
            P(("dp", "expert")),
            P(("dp", "expert"), None, None),
            P(("dp", "expert"), None, None),
            P("expert", None),
        ),
        out_specs=(
            P(("dp", "expert"), None),
            P(("dp", "expert"), None, None),
            P(("dp", "expert"), None, None),
        ),
        check_vma=False,
    )
```

```python
import functools

import jax
import jax.numpy as jnp
from jax import lax
from jax.experimental import pallas as pl
from jax.experimental.pallas import tpu as pltpu
from jax.sharding import PartitionSpec as P

QUERY_HEADS = 12
KEY_VALUE_HEADS = 2
HEAD_SIZE = 128
DEC_DEV = 8
PCH = 128
CONTEXT_LENGTH = 512


def attention_kernel(arrived_only, dt_ref, pt_ref, dl_ref, plen_ref, q_ref, fk_ref, fv_ref, pk_ref, pv_ref, arrived_ref, o_ref):
    f32 = jnp.float32
    bf16 = jnp.bfloat16
    group = QUERY_HEADS // KEY_VALUE_HEADS
    scale = HEAD_SIZE ** (-0.5)
    page_rows = pk_ref.shape[1]
    pages = CONTEXT_LENGTH // page_rows
    nt = (((1,), (1,)), ((), ()))
    lane_pos = lax.broadcasted_iota(jnp.int32, (1, page_rows), 1)
    dec_rows = [[None] * QUERY_HEADS for _ in range(DEC_DEV)]
    requests = [DEC_DEV - 1] if arrived_only else list(range(DEC_DEV - 1))
    for g in range(KEY_VALUE_HEADS):
        lanes = pl.ds(g * HEAD_SIZE, HEAD_SIZE)
        for b in requests:
            length = dl_ref[0, b]
            q = jnp.concatenate(
                [q_ref[pl.ds(b, 1), pl.ds((g * group + j) * HEAD_SIZE, HEAD_SIZE)] for j in range(group)],
                axis=0,
            )
            kf = fk_ref[pl.ds(b, 1), lanes].astype(f32)
            vf = fv_ref[pl.ds(b, 1), lanes].astype(f32)
            w_new = jnp.exp(jnp.sum(q.astype(f32) * kf, axis=-1, keepdims=True) * scale)
            total = w_new
            acc = w_new.astype(bf16).astype(f32) * vf
            for p in range(pages):
                if b < DEC_DEV - 1:
                    page = dt_ref[b, p]
                    k = pk_ref[page, :, lanes]
                    v = pv_ref[page, :, lanes]
                else:
                    k = arrived_ref[pl.ds(p * page_rows, page_rows), lanes]
                    v = arrived_ref[pl.ds(p * page_rows, page_rows), pl.ds(KEY_VALUE_HEADS * HEAD_SIZE + g * HEAD_SIZE, HEAD_SIZE)]
                s = lax.dot_general(q, k, nt, preferred_element_type=f32) * scale
                w = jnp.where(lane_pos + p * page_rows < length, jnp.exp(s), 0.0)
                total = total + jnp.sum(w, axis=-1, keepdims=True)
                acc = acc + jnp.dot(w.astype(bf16), v, preferred_element_type=f32)
            out = acc / total
            for j in range(group):
                dec_rows[b][g * group + j] = out[j : j + 1]
    if arrived_only:
        for h in range(QUERY_HEADS):
            o_ref[:, pl.ds(h * HEAD_SIZE, HEAD_SIZE)] = dec_rows[DEC_DEV - 1][h].astype(o_ref.dtype)
        return
    dec_rows[DEC_DEV - 1] = [jnp.zeros((1, HEAD_SIZE), f32)] * QUERY_HEADS
    prefill_length = plen_ref[0]
    rows = group * PCH
    row_pos = lax.broadcasted_iota(jnp.int32, (rows, page_rows), 0) % PCH
    col_pos = lax.broadcasted_iota(jnp.int32, (rows, page_rows), 1)
    causal = col_pos <= row_pos
    for g in range(KEY_VALUE_HEADS):
        lanes = pl.ds(g * HEAD_SIZE, HEAD_SIZE)
        q = jnp.concatenate(
            [q_ref[:, pl.ds((g * group + j) * HEAD_SIZE, HEAD_SIZE)].astype(f32)[DEC_DEV:] for j in range(group)],
            axis=0,
        ).astype(bf16)
        kb = fk_ref[:, lanes].astype(f32)[DEC_DEV:].astype(bf16)
        vb = fv_ref[:, lanes].astype(f32)[DEC_DEV:].astype(bf16)
        s = lax.dot_general(q, kb, nt, preferred_element_type=f32) * scale
        w = jnp.where(causal, jnp.exp(s), 0.0)
        total = jnp.sum(w, axis=-1, keepdims=True)
        acc = jnp.dot(w.astype(bf16), vb, preferred_element_type=f32)
        for p in range(pages):
            page = pt_ref[0, p]
            k = pk_ref[page, :, lanes]
            v = pv_ref[page, :, lanes]
            s = lax.dot_general(q, k, nt, preferred_element_type=f32) * scale
            w = jnp.where(col_pos + p * page_rows < prefill_length, jnp.exp(s), 0.0)
            total = total + jnp.sum(w, axis=-1, keepdims=True)
            acc = acc + jnp.dot(w.astype(bf16), v, preferred_element_type=f32)
        out = acc / total
        for j in range(group):
            h = g * group + j
            dec_col = jnp.concatenate([dec_rows[b][h] for b in range(DEC_DEV)], axis=0)
            o_ref[:, pl.ds(h * HEAD_SIZE, HEAD_SIZE)] = jnp.concatenate(
                [dec_col, out[j * PCH : (j + 1) * PCH]], axis=0
            ).astype(o_ref.dtype)


def paged_attention(arrived_only, decode_table, prefill_table, decode_len, prefill_len, queries, fresh_keys, fresh_values, paged_keys, paged_values, arrived):
    smem = pl.BlockSpec(memory_space=pltpu.SMEM)
    vmem = pl.BlockSpec(memory_space=pltpu.VMEM)
    rows = 1 if arrived_only else queries.shape[0]
    return pl.pallas_call(
        functools.partial(attention_kernel, arrived_only),
        out_shape=jax.ShapeDtypeStruct((rows, queries.shape[1]), queries.dtype),
        in_specs=[smem] * 4 + [vmem] * 6,
        out_specs=vmem,
    )(decode_table, prefill_table, decode_len, prefill_len, queries, fresh_keys, fresh_values, paged_keys, paged_values, arrived)


def capacity_for(token_count, route_count, expert_count):
    return min(token_count, (token_count * route_count // expert_count * 3 // 2 + 7) // 8 * 8)


def page_lookup(table, pool_flat):
    pool_count = pool_flat.shape[0]
    selector = (table[..., None] == jnp.arange(pool_count, dtype=jnp.int32)).astype(jnp.bfloat16)
    return jnp.einsum(
        "...p,pk->...k", selector, pool_flat, preferred_element_type=jnp.float32
    ).astype(jnp.bfloat16)


def on_device(
    queries,
    fresh_keys,
    fresh_values,
    residual,
    norm_gain,
    out_weight,
    router_weight,
    gate_weight,
    up_weight,
    down_weight,
    expert_ids,
    paged_keys,
    paged_values,
    decode_table,
    prefill_table,
    decode_len,
    prefill_len,
    departing_keys,
    departing_values,
    destination,
):
    width_total = KEY_VALUE_HEADS * HEAD_SIZE
    target_row = destination[0]
    dp_count = target_row.shape[0]
    rows_total = departing_keys.shape[1]
    chunk_rows = rows_total // dp_count
    both = jnp.concatenate([departing_keys[0], departing_values[0]], axis=-1)
    both = both.reshape(dp_count, chunk_rows, 2 * width_total)
    spread = lax.all_to_all(both, "dp", split_axis=0, concat_axis=0, tiled=True)
    sources = jnp.sum(
        jnp.where(
            target_row[None, :] == jnp.arange(dp_count, dtype=jnp.int32)[:, None],
            jnp.arange(dp_count, dtype=jnp.int32)[None, :],
            0,
        ),
        axis=1,
    )
    routed = jnp.take(spread, sources, axis=0)
    gathered = lax.all_to_all(routed, "dp", split_axis=0, concat_axis=0, tiled=True)
    gathered = gathered.reshape(rows_total, 2 * width_total)
    take_keys = gathered[None, :, :width_total]
    take_values = gathered[None, :, width_total:]
    token_count = queries.shape[0]
    table_args = (decode_table, prefill_table, decode_len, prefill_len, queries, fresh_keys, fresh_values)
    attended = paged_attention(False, *table_args, paged_keys, paged_values, both)
    attended_last = paged_attention(True, *table_args, paged_keys, paged_values, gathered)
    attended = lax.dynamic_update_slice(attended, attended_last, (DEC_DEV - 1, 0))
    hidden = residual.astype(jnp.float32) + jnp.dot(
        attended, out_weight, preferred_element_type=jnp.float32
    )
    variance = jnp.mean(hidden * hidden, axis=-1, keepdims=True)
    normed = (hidden * lax.rsqrt(variance + 1e-06) * norm_gain).astype(jnp.bfloat16)
    logits = jnp.dot(normed, router_weight, preferred_element_type=jnp.float32)
    expert_count = router_weight.shape[1]
    expert_range = jnp.arange(expert_count, dtype=jnp.int32)
    chosen = jnp.sum(
        jnp.where(expert_ids[:, :, None] == expert_range, logits[:, None, :], 0.0), axis=-1
    )
    chosen = jax.nn.sigmoid(chosen)
    gates = chosen / jnp.sum(chosen, axis=1, keepdims=True)
    route_count = expert_ids.shape[1]
    capacity = capacity_for(token_count, route_count, expert_count)
    slot_total = expert_count * capacity
    flat_ids = expert_ids.T.reshape(-1)
    hits = (flat_ids[:, None] == expert_range[None, :]).astype(jnp.int32)
    ranks = jnp.sum((jnp.cumsum(hits, axis=0) - 1) * hits, axis=1)
    slot_of_route = flat_ids * capacity + ranks
    route_slots = (
        slot_of_route[:, None] == jnp.arange(slot_total, dtype=jnp.int32)[None, :]
    ).astype(jnp.bfloat16)
    token_slots = jnp.sum(route_slots.reshape(route_count, token_count, slot_total), axis=0)
    outgoing = jnp.einsum(
        "ts,td->sd", token_slots, normed, preferred_element_type=jnp.float32
    ).astype(jnp.bfloat16)
    outgoing = outgoing.reshape(expert_count, capacity, normed.shape[1])
    received = lax.all_to_all(outgoing, "expert", split_axis=0, concat_axis=0, tiled=True)
    gate_part = jnp.einsum(
        "scd,df->scf", received, gate_weight[0], preferred_element_type=jnp.float32
    )
    up_part = jnp.einsum("scd,df->scf", received, up_weight[0], preferred_element_type=jnp.float32)
    inner = lax.optimization_barrier((jax.nn.relu(gate_part) * up_part).astype(jnp.bfloat16))
    processed = jnp.einsum(
        "scf,fd->scd", inner, down_weight[0], preferred_element_type=jnp.float32
    ).astype(jnp.bfloat16)
    returned = lax.all_to_all(processed, "expert", split_axis=0, concat_axis=0, tiled=True)
    returned_flat = returned.reshape(slot_total, returned.shape[2])
    route_out = jnp.dot(route_slots, returned_flat, preferred_element_type=jnp.float32).astype(
        jnp.bfloat16
    ).reshape(route_count, token_count, -1)
    mixture = jnp.sum(gates.T[:, :, None] * route_out.astype(jnp.float32), axis=0)
    layer_out = (hidden + mixture).astype(jnp.bfloat16)
    last_len = decode_len[0, DEC_DEV - 1]
    moved_keys = lax.dynamic_update_slice(
        take_keys,
        fresh_keys[DEC_DEV - 1][None, None],
        (jnp.zeros((), jnp.int32), last_len, jnp.zeros((), jnp.int32)),
    )
    moved_values = lax.dynamic_update_slice(
        take_values,
        fresh_values[DEC_DEV - 1][None, None],
        (jnp.zeros((), jnp.int32), last_len, jnp.zeros((), jnp.int32)),
    )
    return (layer_out, moved_keys, moved_values)


def solution(mesh):
    return jax.shard_map(
        on_device,
        mesh=mesh,
        in_specs=(
            P(("dp", "expert"), None),
            P(("dp", "expert"), None),
            P(("dp", "expert"), None),
            P(("dp", "expert"), None),
            P(),
            P(),
            P(),
            P("expert", None, None),
            P("expert", None, None),
            P("expert", None, None),
            P(("dp", "expert"), None),
            P(("dp", "expert"), None, None),
            P(("dp", "expert"), None, None),
            P(("dp", "expert"), None),
            P(("dp", "expert"), None),
            P(("dp", "expert"), None),
            P(("dp", "expert")),
            P(("dp", "expert"), None, None),
            P(("dp", "expert"), None, None),
            P("expert", None),
        ),
        out_specs=(
            P(("dp", "expert"), None),
            P(("dp", "expert"), None, None),
            P(("dp", "expert"), None, None),
        ),
        check_vma=False,
    )
```

```python
import functools

import jax
import jax.numpy as jnp
from jax import lax
from jax.experimental import pallas as pl
from jax.experimental.pallas import tpu as pltpu
from jax.sharding import PartitionSpec as P

QUERY_HEADS = 12
KEY_VALUE_HEADS = 2
HEAD_SIZE = 128
DEC_DEV = 8
PCH = 128
CONTEXT_LENGTH = 512
PAGE_TOKENS = 128


def attention_kernel(arrived_only, dt_ref, pt_ref, dl_ref, plen_ref, q_ref, fk_ref, fv_ref, pk_ref, pv_ref, arrived_ref, o_ref):
    f32 = jnp.float32
    bf16 = jnp.bfloat16
    group = QUERY_HEADS // KEY_VALUE_HEADS
    scale = HEAD_SIZE ** (-0.5)
    page_rows = PAGE_TOKENS if pk_ref is None else pk_ref.shape[1]
    pages = CONTEXT_LENGTH // page_rows
    nt = (((1,), (1,)), ((), ()))
    lane_pos = lax.broadcasted_iota(jnp.int32, (1, page_rows), 1)
    dec_rows = [[None] * QUERY_HEADS for _ in range(DEC_DEV)]
    requests = [DEC_DEV - 1] if arrived_only else list(range(DEC_DEV - 1))
    for g in range(KEY_VALUE_HEADS):
        lanes = pl.ds(g * HEAD_SIZE, HEAD_SIZE)
        for b in requests:
            length = dl_ref[0, b]
            q = jnp.concatenate(
                [q_ref[pl.ds(b, 1), pl.ds((g * group + j) * HEAD_SIZE, HEAD_SIZE)] for j in range(group)],
                axis=0,
            )
            kf = fk_ref[pl.ds(b, 1), lanes].astype(f32)
            vf = fv_ref[pl.ds(b, 1), lanes].astype(f32)
            w_new = jnp.exp(jnp.sum(q.astype(f32) * kf, axis=-1, keepdims=True) * scale)
            total = w_new
            acc = w_new.astype(bf16).astype(f32) * vf
            for p in range(pages):
                if b < DEC_DEV - 1:
                    page = dt_ref[b, p]
                    k = pk_ref[page, :, lanes]
                    v = pv_ref[page, :, lanes]
                else:
                    k = arrived_ref[pl.ds(p * page_rows, page_rows), lanes]
                    v = arrived_ref[pl.ds(p * page_rows, page_rows), pl.ds(KEY_VALUE_HEADS * HEAD_SIZE + g * HEAD_SIZE, HEAD_SIZE)]
                s = lax.dot_general(q, k, nt, preferred_element_type=f32) * scale
                w = jnp.where(lane_pos + p * page_rows < length, jnp.exp(s), 0.0)
                total = total + jnp.sum(w, axis=-1, keepdims=True)
                acc = acc + jnp.dot(w.astype(bf16), v, preferred_element_type=f32)
            out = acc / total
            for j in range(group):
                dec_rows[b][g * group + j] = out[j : j + 1]
    if arrived_only:
        for h in range(QUERY_HEADS):
            o_ref[:, pl.ds(h * HEAD_SIZE, HEAD_SIZE)] = dec_rows[DEC_DEV - 1][h].astype(o_ref.dtype)
        return
    dec_rows[DEC_DEV - 1] = [jnp.zeros((1, HEAD_SIZE), f32)] * QUERY_HEADS
    prefill_length = plen_ref[0]
    rows = group * PCH
    row_pos = lax.broadcasted_iota(jnp.int32, (rows, page_rows), 0) % PCH
    col_pos = lax.broadcasted_iota(jnp.int32, (rows, page_rows), 1)
    causal = col_pos <= row_pos
    for g in range(KEY_VALUE_HEADS):
        lanes = pl.ds(g * HEAD_SIZE, HEAD_SIZE)
        q = jnp.concatenate(
            [q_ref[:, pl.ds((g * group + j) * HEAD_SIZE, HEAD_SIZE)].astype(f32)[DEC_DEV:] for j in range(group)],
            axis=0,
        ).astype(bf16)
        kb = fk_ref[:, lanes].astype(f32)[DEC_DEV:].astype(bf16)
        vb = fv_ref[:, lanes].astype(f32)[DEC_DEV:].astype(bf16)
        s = lax.dot_general(q, kb, nt, preferred_element_type=f32) * scale
        w = jnp.where(causal, jnp.exp(s), 0.0)
        total = jnp.sum(w, axis=-1, keepdims=True)
        acc = jnp.dot(w.astype(bf16), vb, preferred_element_type=f32)
        for p in range(pages):
            page = pt_ref[0, p]
            k = pk_ref[page, :, lanes]
            v = pv_ref[page, :, lanes]
            s = lax.dot_general(q, k, nt, preferred_element_type=f32) * scale
            w = jnp.where(col_pos + p * page_rows < prefill_length, jnp.exp(s), 0.0)
            total = total + jnp.sum(w, axis=-1, keepdims=True)
            acc = acc + jnp.dot(w.astype(bf16), v, preferred_element_type=f32)
        out = acc / total
        for j in range(group):
            h = g * group + j
            dec_col = jnp.concatenate([dec_rows[b][h] for b in range(DEC_DEV)], axis=0)
            o_ref[:, pl.ds(h * HEAD_SIZE, HEAD_SIZE)] = jnp.concatenate(
                [dec_col, out[j * PCH : (j + 1) * PCH]], axis=0
            ).astype(o_ref.dtype)


def paged_attention(arrived_only, decode_table, prefill_table, decode_len, prefill_len, queries, fresh_keys, fresh_values, paged_keys, paged_values, arrived):
    smem = pl.BlockSpec(memory_space=pltpu.SMEM)
    vmem = pl.BlockSpec(memory_space=pltpu.VMEM)
    rows = 1 if arrived_only else queries.shape[0]
    return pl.pallas_call(
        functools.partial(attention_kernel, arrived_only),
        out_shape=jax.ShapeDtypeStruct((rows, queries.shape[1]), queries.dtype),
        in_specs=[smem] * 4 + [vmem] * 6,
        out_specs=vmem,
    )(decode_table, prefill_table, decode_len, prefill_len, queries, fresh_keys, fresh_values, paged_keys, paged_values, arrived)


def last_request_kernel(dl_ref, q_ref, fk_ref, fv_ref, arrived_ref, o_ref):
    attention_kernel(True, None, None, dl_ref, None, q_ref, fk_ref, fv_ref, None, None, arrived_ref, o_ref)


def last_request_attention(decode_len, queries, fresh_keys, fresh_values, arrived):
    def rows_of(width):
        return pl.BlockSpec((DEC_DEV, width), lambda i: (0, 0))

    return pl.pallas_call(
        last_request_kernel,
        out_shape=jax.ShapeDtypeStruct((1, queries.shape[1]), queries.dtype),
        grid=(1,),
        in_specs=[
            pl.BlockSpec(memory_space=pltpu.SMEM),
            rows_of(queries.shape[1]),
            rows_of(fresh_keys.shape[1]),
            rows_of(fresh_values.shape[1]),
            pl.BlockSpec(arrived.shape, lambda i: (0, 0)),
        ],
        out_specs=pl.BlockSpec((1, queries.shape[1]), lambda i: (0, 0)),
    )(decode_len, queries, fresh_keys, fresh_values, arrived)


def capacity_for(token_count, route_count, expert_count):
    return min(token_count, (token_count * route_count // expert_count * 3 // 2 + 7) // 8 * 8)


def page_lookup(table, pool_flat):
    pool_count = pool_flat.shape[0]
    selector = (table[..., None] == jnp.arange(pool_count, dtype=jnp.int32)).astype(jnp.bfloat16)
    return jnp.einsum(
        "...p,pk->...k", selector, pool_flat, preferred_element_type=jnp.float32
    ).astype(jnp.bfloat16)


def on_device(
    queries,
    fresh_keys,
    fresh_values,
    residual,
    norm_gain,
    out_weight,
    router_weight,
    gate_weight,
    up_weight,
    down_weight,
    expert_ids,
    paged_keys,
    paged_values,
    decode_table,
    prefill_table,
    decode_len,
    prefill_len,
    departing_keys,
    departing_values,
    destination,
):
    width_total = KEY_VALUE_HEADS * HEAD_SIZE
    target_row = destination[0]
    dp_count = target_row.shape[0]
    rows_total = departing_keys.shape[1]
    chunk_rows = rows_total // dp_count
    both = jnp.concatenate([departing_keys[0], departing_values[0]], axis=-1)
    both = both.reshape(dp_count, chunk_rows, 2 * width_total)
    spread = lax.all_to_all(both, "dp", split_axis=0, concat_axis=0, tiled=True)
    sources = jnp.sum(
        jnp.where(
            target_row[None, :] == jnp.arange(dp_count, dtype=jnp.int32)[:, None],
            jnp.arange(dp_count, dtype=jnp.int32)[None, :],
            0,
        ),
        axis=1,
    )
    routed = jnp.take(spread, sources, axis=0)
    gathered = lax.all_to_all(routed, "dp", split_axis=0, concat_axis=0, tiled=True)
    gathered = gathered.reshape(rows_total, 2 * width_total)
    take_keys = gathered[None, :, :width_total]
    take_values = gathered[None, :, width_total:]
    token_count = queries.shape[0]
    table_args = (decode_table, prefill_table, decode_len, prefill_len, queries, fresh_keys, fresh_values)
    attended = paged_attention(False, *table_args, paged_keys, paged_values, both)
    attended_last = last_request_attention(decode_len, queries, fresh_keys, fresh_values, gathered)
    attended = lax.dynamic_update_slice(attended, attended_last, (DEC_DEV - 1, 0))
    hidden = residual.astype(jnp.float32) + jnp.dot(
        attended, out_weight, preferred_element_type=jnp.float32
    )
    variance = jnp.mean(hidden * hidden, axis=-1, keepdims=True)
    normed = (hidden * lax.rsqrt(variance + 1e-06) * norm_gain).astype(jnp.bfloat16)
    logits = jnp.dot(normed, router_weight, preferred_element_type=jnp.float32)
    expert_count = router_weight.shape[1]
    expert_range = jnp.arange(expert_count, dtype=jnp.int32)
    chosen = jnp.sum(
        jnp.where(expert_ids[:, :, None] == expert_range, logits[:, None, :], 0.0), axis=-1
    )
    chosen = jax.nn.sigmoid(chosen)
    gates = chosen / jnp.sum(chosen, axis=1, keepdims=True)
    route_count = expert_ids.shape[1]
    capacity = capacity_for(token_count, route_count, expert_count)
    slot_total = expert_count * capacity
    flat_ids = expert_ids.T.reshape(-1)
    hits = (flat_ids[:, None] == expert_range[None, :]).astype(jnp.int32)
    ranks = jnp.sum((jnp.cumsum(hits, axis=0) - 1) * hits, axis=1)
    slot_of_route = flat_ids * capacity + ranks
    route_slots = (
        slot_of_route[:, None] == jnp.arange(slot_total, dtype=jnp.int32)[None, :]
    ).astype(jnp.bfloat16)
    token_slots = jnp.sum(route_slots.reshape(route_count, token_count, slot_total), axis=0)
    outgoing = jnp.einsum(
        "ts,td->sd", token_slots, normed, preferred_element_type=jnp.float32
    ).astype(jnp.bfloat16)
    outgoing = outgoing.reshape(expert_count, capacity, normed.shape[1])
    received = lax.all_to_all(outgoing, "expert", split_axis=0, concat_axis=0, tiled=True)
    gate_part = jnp.einsum(
        "scd,df->scf", received, gate_weight[0], preferred_element_type=jnp.float32
    )
    up_part = jnp.einsum("scd,df->scf", received, up_weight[0], preferred_element_type=jnp.float32)
    inner = lax.optimization_barrier((jax.nn.relu(gate_part) * up_part).astype(jnp.bfloat16))
    processed = jnp.einsum(
        "scf,fd->scd", inner, down_weight[0], preferred_element_type=jnp.float32
    ).astype(jnp.bfloat16)
    returned = lax.all_to_all(processed, "expert", split_axis=0, concat_axis=0, tiled=True)
    returned_flat = returned.reshape(slot_total, returned.shape[2])
    route_out = jnp.dot(route_slots, returned_flat, preferred_element_type=jnp.float32).astype(
        jnp.bfloat16
    ).reshape(route_count, token_count, -1)
    mixture = jnp.sum(gates.T[:, :, None] * route_out.astype(jnp.float32), axis=0)
    layer_out = (hidden + mixture).astype(jnp.bfloat16)
    last_len = decode_len[0, DEC_DEV - 1]
    moved_keys = lax.dynamic_update_slice(
        take_keys,
        fresh_keys[DEC_DEV - 1][None, None],
        (jnp.zeros((), jnp.int32), last_len, jnp.zeros((), jnp.int32)),
    )
    moved_values = lax.dynamic_update_slice(
        take_values,
        fresh_values[DEC_DEV - 1][None, None],
        (jnp.zeros((), jnp.int32), last_len, jnp.zeros((), jnp.int32)),
    )
    return (layer_out, moved_keys, moved_values)


def solution(mesh):
    return jax.shard_map(
        on_device,
        mesh=mesh,
        in_specs=(
            P(("dp", "expert"), None),
            P(("dp", "expert"), None),
            P(("dp", "expert"), None),
            P(("dp", "expert"), None),
            P(),
            P(),
            P(),
            P("expert", None, None),
            P("expert", None, None),
            P("expert", None, None),
            P(("dp", "expert"), None),
            P(("dp", "expert"), None, None),
            P(("dp", "expert"), None, None),
            P(("dp", "expert"), None),
            P(("dp", "expert"), None),
            P(("dp", "expert"), None),
            P(("dp", "expert")),
            P(("dp", "expert"), None, None),
            P(("dp", "expert"), None, None),
            P("expert", None),
        ),
        out_specs=(
            P(("dp", "expert"), None),
            P(("dp", "expert"), None, None),
            P(("dp", "expert"), None, None),
        ),
        check_vma=False,
    )
```

```python
import functools

import jax
import jax.numpy as jnp
from jax import lax
from jax.experimental import pallas as pl
from jax.experimental.pallas import tpu as pltpu
from jax.sharding import PartitionSpec as P

QUERY_HEADS = 12
KEY_VALUE_HEADS = 2
HEAD_SIZE = 128
DEC_DEV = 8
PCH = 128
CONTEXT_LENGTH = 512
PAGE_TOKENS = 128


def attention_kernel(arrived_only, dt_ref, pt_ref, dl_ref, plen_ref, q_ref, fk_ref, fv_ref, pk_ref, pv_ref, arrived_ref, o_ref, base_ref=None):
    f32 = jnp.float32
    bf16 = jnp.bfloat16
    group = QUERY_HEADS // KEY_VALUE_HEADS
    scale = HEAD_SIZE ** (-0.5)
    page_rows = PAGE_TOKENS if pk_ref is None else pk_ref.shape[1]
    pages = CONTEXT_LENGTH // page_rows
    nt = (((1,), (1,)), ((), ()))
    lane_pos = lax.broadcasted_iota(jnp.int32, (1, page_rows), 1)
    dec_rows = [[None] * QUERY_HEADS for _ in range(DEC_DEV)]
    requests = [DEC_DEV - 1] if arrived_only else list(range(DEC_DEV - 1))
    for g in range(KEY_VALUE_HEADS):
        lanes = pl.ds(g * HEAD_SIZE, HEAD_SIZE)
        for b in requests:
            length = dl_ref[0, b]
            q = jnp.concatenate(
                [q_ref[pl.ds(b, 1), pl.ds((g * group + j) * HEAD_SIZE, HEAD_SIZE)] for j in range(group)],
                axis=0,
            )
            kf = fk_ref[pl.ds(b, 1), lanes].astype(f32)
            vf = fv_ref[pl.ds(b, 1), lanes].astype(f32)
            w_new = jnp.exp(jnp.sum(q.astype(f32) * kf, axis=-1, keepdims=True) * scale)
            total = w_new
            acc = w_new.astype(bf16).astype(f32) * vf
            for p in range(pages):
                if b < DEC_DEV - 1:
                    page = dt_ref[b, p]
                    k = pk_ref[page, :, lanes]
                    v = pv_ref[page, :, lanes]
                else:
                    k = arrived_ref[pl.ds(p * page_rows, page_rows), lanes]
                    v = arrived_ref[pl.ds(p * page_rows, page_rows), pl.ds(KEY_VALUE_HEADS * HEAD_SIZE + g * HEAD_SIZE, HEAD_SIZE)]
                s = lax.dot_general(q, k, nt, preferred_element_type=f32) * scale
                w = jnp.where(lane_pos + p * page_rows < length, jnp.exp(s), 0.0)
                total = total + jnp.sum(w, axis=-1, keepdims=True)
                acc = acc + jnp.dot(w.astype(bf16), v, preferred_element_type=f32)
            out = acc / total
            for j in range(group):
                dec_rows[b][g * group + j] = out[j : j + 1]
    if arrived_only:
        row = jnp.concatenate(dec_rows[DEC_DEV - 1], axis=1)
        kept = base_ref[...].astype(f32)[: DEC_DEV - 1]
        o_ref[...] = jnp.concatenate([kept, row], axis=0).astype(o_ref.dtype)
        return
    dec_rows[DEC_DEV - 1] = [jnp.zeros((1, HEAD_SIZE), f32)] * QUERY_HEADS
    prefill_length = plen_ref[0]
    rows = group * PCH
    row_pos = lax.broadcasted_iota(jnp.int32, (rows, page_rows), 0) % PCH
    col_pos = lax.broadcasted_iota(jnp.int32, (rows, page_rows), 1)
    causal = col_pos <= row_pos
    for g in range(KEY_VALUE_HEADS):
        lanes = pl.ds(g * HEAD_SIZE, HEAD_SIZE)
        q = jnp.concatenate(
            [q_ref[:, pl.ds((g * group + j) * HEAD_SIZE, HEAD_SIZE)].astype(f32)[DEC_DEV:] for j in range(group)],
            axis=0,
        ).astype(bf16)
        kb = fk_ref[:, lanes].astype(f32)[DEC_DEV:].astype(bf16)
        vb = fv_ref[:, lanes].astype(f32)[DEC_DEV:].astype(bf16)
        s = lax.dot_general(q, kb, nt, preferred_element_type=f32) * scale
        w = jnp.where(causal, jnp.exp(s), 0.0)
        total = jnp.sum(w, axis=-1, keepdims=True)
        acc = jnp.dot(w.astype(bf16), vb, preferred_element_type=f32)
        for p in range(pages):
            page = pt_ref[0, p]
            k = pk_ref[page, :, lanes]
            v = pv_ref[page, :, lanes]
            s = lax.dot_general(q, k, nt, preferred_element_type=f32) * scale
            w = jnp.where(col_pos + p * page_rows < prefill_length, jnp.exp(s), 0.0)
            total = total + jnp.sum(w, axis=-1, keepdims=True)
            acc = acc + jnp.dot(w.astype(bf16), v, preferred_element_type=f32)
        out = acc / total
        for j in range(group):
            h = g * group + j
            dec_col = jnp.concatenate([dec_rows[b][h] for b in range(DEC_DEV)], axis=0)
            o_ref[:, pl.ds(h * HEAD_SIZE, HEAD_SIZE)] = jnp.concatenate(
                [dec_col, out[j * PCH : (j + 1) * PCH]], axis=0
            ).astype(o_ref.dtype)


def paged_attention(arrived_only, decode_table, prefill_table, decode_len, prefill_len, queries, fresh_keys, fresh_values, paged_keys, paged_values, arrived):
    smem = pl.BlockSpec(memory_space=pltpu.SMEM)
    vmem = pl.BlockSpec(memory_space=pltpu.VMEM)
    rows = 1 if arrived_only else queries.shape[0]
    return pl.pallas_call(
        functools.partial(attention_kernel, arrived_only),
        out_shape=jax.ShapeDtypeStruct((rows, queries.shape[1]), queries.dtype),
        in_specs=[smem] * 4 + [vmem] * 6,
        out_specs=vmem,
    )(decode_table, prefill_table, decode_len, prefill_len, queries, fresh_keys, fresh_values, paged_keys, paged_values, arrived)


def last_request_kernel(dl_ref, q_ref, fk_ref, fv_ref, arrived_ref, base_ref, o_ref):
    attention_kernel(
        True, None, None, dl_ref, None, q_ref, fk_ref, fv_ref, None, None, arrived_ref, o_ref, base_ref
    )


def last_request_attention(decode_len, queries, fresh_keys, fresh_values, arrived, base):
    def rows_of(width):
        return pl.BlockSpec((DEC_DEV, width), lambda i: (0, 0))

    return pl.pallas_call(
        last_request_kernel,
        out_shape=jax.ShapeDtypeStruct(base.shape, base.dtype),
        grid=(1,),
        in_specs=[
            pl.BlockSpec(memory_space=pltpu.SMEM),
            rows_of(queries.shape[1]),
            rows_of(fresh_keys.shape[1]),
            rows_of(fresh_values.shape[1]),
            pl.BlockSpec(arrived.shape, lambda i: (0, 0)),
            rows_of(base.shape[1]),
        ],
        out_specs=rows_of(base.shape[1]),
        input_output_aliases={5: 0},
    )(decode_len, queries, fresh_keys, fresh_values, arrived, base)


def capacity_for(token_count, route_count, expert_count):
    return min(token_count, (token_count * route_count // expert_count * 3 // 2 + 7) // 8 * 8)


def page_lookup(table, pool_flat):
    pool_count = pool_flat.shape[0]
    selector = (table[..., None] == jnp.arange(pool_count, dtype=jnp.int32)).astype(jnp.bfloat16)
    return jnp.einsum(
        "...p,pk->...k", selector, pool_flat, preferred_element_type=jnp.float32
    ).astype(jnp.bfloat16)


def on_device(
    queries,
    fresh_keys,
    fresh_values,
    residual,
    norm_gain,
    out_weight,
    router_weight,
    gate_weight,
    up_weight,
    down_weight,
    expert_ids,
    paged_keys,
    paged_values,
    decode_table,
    prefill_table,
    decode_len,
    prefill_len,
    departing_keys,
    departing_values,
    destination,
):
    width_total = KEY_VALUE_HEADS * HEAD_SIZE
    target_row = destination[0]
    dp_count = target_row.shape[0]
    rows_total = departing_keys.shape[1]
    chunk_rows = rows_total // dp_count
    both = jnp.concatenate([departing_keys[0], departing_values[0]], axis=-1)
    both = both.reshape(dp_count, chunk_rows, 2 * width_total)
    spread = lax.all_to_all(both, "dp", split_axis=0, concat_axis=0, tiled=True)
    sources = jnp.sum(
        jnp.where(
            target_row[None, :] == jnp.arange(dp_count, dtype=jnp.int32)[:, None],
            jnp.arange(dp_count, dtype=jnp.int32)[None, :],
            0,
        ),
        axis=1,
    )
    routed = jnp.take(spread, sources, axis=0)
    gathered = lax.all_to_all(routed, "dp", split_axis=0, concat_axis=0, tiled=True)
    gathered = gathered.reshape(rows_total, 2 * width_total)
    take_keys = gathered[None, :, :width_total]
    take_values = gathered[None, :, width_total:]
    token_count = queries.shape[0]
    table_args = (decode_table, prefill_table, decode_len, prefill_len, queries, fresh_keys, fresh_values)
    attended = paged_attention(False, *table_args, paged_keys, paged_values, both)
    attended = last_request_attention(decode_len, queries, fresh_keys, fresh_values, gathered, attended)
    hidden = residual.astype(jnp.float32) + jnp.dot(
        attended, out_weight, preferred_element_type=jnp.float32
    )
    variance = jnp.mean(hidden * hidden, axis=-1, keepdims=True)
    normed = (hidden * lax.rsqrt(variance + 1e-06) * norm_gain).astype(jnp.bfloat16)
    logits = jnp.dot(normed, router_weight, preferred_element_type=jnp.float32)
    expert_count = router_weight.shape[1]
    expert_range = jnp.arange(expert_count, dtype=jnp.int32)
    chosen = jnp.sum(
        jnp.where(expert_ids[:, :, None] == expert_range, logits[:, None, :], 0.0), axis=-1
    )
    chosen = jax.nn.sigmoid(chosen)
    gates = chosen / jnp.sum(chosen, axis=1, keepdims=True)
    route_count = expert_ids.shape[1]
    capacity = capacity_for(token_count, route_count, expert_count)
    slot_total = expert_count * capacity
    flat_ids = expert_ids.T.reshape(-1)
    hits = (flat_ids[:, None] == expert_range[None, :]).astype(jnp.int32)
    ranks = jnp.sum((jnp.cumsum(hits, axis=0) - 1) * hits, axis=1)
    slot_of_route = flat_ids * capacity + ranks
    route_slots = (
        slot_of_route[:, None] == jnp.arange(slot_total, dtype=jnp.int32)[None, :]
    ).astype(jnp.bfloat16)
    token_slots = jnp.sum(route_slots.reshape(route_count, token_count, slot_total), axis=0)
    outgoing = jnp.einsum(
        "ts,td->sd", token_slots, normed, preferred_element_type=jnp.float32
    ).astype(jnp.bfloat16)
    outgoing = outgoing.reshape(expert_count, capacity, normed.shape[1])
    received = lax.all_to_all(outgoing, "expert", split_axis=0, concat_axis=0, tiled=True)
    gate_part = jnp.einsum(
        "scd,df->scf", received, gate_weight[0], preferred_element_type=jnp.float32
    )
    up_part = jnp.einsum("scd,df->scf", received, up_weight[0], preferred_element_type=jnp.float32)
    inner = lax.optimization_barrier((jax.nn.relu(gate_part) * up_part).astype(jnp.bfloat16))
    processed = jnp.einsum(
        "scf,fd->scd", inner, down_weight[0], preferred_element_type=jnp.float32
    ).astype(jnp.bfloat16)
    returned = lax.all_to_all(processed, "expert", split_axis=0, concat_axis=0, tiled=True)
    returned_flat = returned.reshape(slot_total, returned.shape[2])
    route_out = jnp.dot(route_slots, returned_flat, preferred_element_type=jnp.float32).astype(
        jnp.bfloat16
    ).reshape(route_count, token_count, -1)
    mixture = jnp.sum(gates.T[:, :, None] * route_out.astype(jnp.float32), axis=0)
    layer_out = (hidden + mixture).astype(jnp.bfloat16)
    last_len = decode_len[0, DEC_DEV - 1]
    moved_keys = lax.dynamic_update_slice(
        take_keys,
        fresh_keys[DEC_DEV - 1][None, None],
        (jnp.zeros((), jnp.int32), last_len, jnp.zeros((), jnp.int32)),
    )
    moved_values = lax.dynamic_update_slice(
        take_values,
        fresh_values[DEC_DEV - 1][None, None],
        (jnp.zeros((), jnp.int32), last_len, jnp.zeros((), jnp.int32)),
    )
    return (layer_out, moved_keys, moved_values)


def solution(mesh):
    return jax.shard_map(
        on_device,
        mesh=mesh,
        in_specs=(
            P(("dp", "expert"), None),
            P(("dp", "expert"), None),
            P(("dp", "expert"), None),
            P(("dp", "expert"), None),
            P(),
            P(),
            P(),
            P("expert", None, None),
            P("expert", None, None),
            P("expert", None, None),
            P(("dp", "expert"), None),
            P(("dp", "expert"), None, None),
            P(("dp", "expert"), None, None),
            P(("dp", "expert"), None),
            P(("dp", "expert"), None),
            P(("dp", "expert"), None),
            P(("dp", "expert")),
            P(("dp", "expert"), None, None),
            P(("dp", "expert"), None, None),
            P("expert", None),
        ),
        out_specs=(
            P(("dp", "expert"), None),
            P(("dp", "expert"), None, None),
            P(("dp", "expert"), None, None),
        ),
        check_vma=False,
    )
```

```python
import functools

import jax
import jax.numpy as jnp
from jax import lax
from jax.experimental import pallas as pl
from jax.experimental.pallas import tpu as pltpu
from jax.sharding import PartitionSpec as P

QUERY_HEADS = 12
KEY_VALUE_HEADS = 2
HEAD_SIZE = 128
DEC_DEV = 8
PCH = 128
CONTEXT_LENGTH = 512
PAGE_TOKENS = 128


def attention_kernel(arrived_only, dt_ref, pt_ref, dl_ref, plen_ref, q_ref, fk_ref, fv_ref, pk_ref, pv_ref, arrived_ref, o_ref, base_ref=None):
    f32 = jnp.float32
    bf16 = jnp.bfloat16
    group = QUERY_HEADS // KEY_VALUE_HEADS
    scale = HEAD_SIZE ** (-0.5)
    page_rows = PAGE_TOKENS if pk_ref is None else pk_ref.shape[1]
    pages = CONTEXT_LENGTH // page_rows
    nt = (((1,), (1,)), ((), ()))
    lane_pos = lax.broadcasted_iota(jnp.int32, (1, page_rows), 1)
    dec_rows = [[None] * QUERY_HEADS for _ in range(DEC_DEV)]
    requests = [DEC_DEV - 1] if arrived_only else list(range(DEC_DEV - 1))
    for g in range(KEY_VALUE_HEADS):
        lanes = pl.ds(g * HEAD_SIZE, HEAD_SIZE)
        for b in requests:
            length = dl_ref[0, b]
            q = jnp.concatenate(
                [q_ref[pl.ds(b, 1), pl.ds((g * group + j) * HEAD_SIZE, HEAD_SIZE)] for j in range(group)],
                axis=0,
            )
            kf = fk_ref[pl.ds(b, 1), lanes].astype(f32)
            vf = fv_ref[pl.ds(b, 1), lanes].astype(f32)
            w_new = jnp.exp(jnp.sum(q.astype(f32) * kf, axis=-1, keepdims=True) * scale)
            total = w_new
            acc = w_new.astype(bf16).astype(f32) * vf
            for p in range(pages):
                if b < DEC_DEV - 1:
                    page = dt_ref[b, p]
                    k = pk_ref[page, :, lanes]
                    v = pv_ref[page, :, lanes]
                else:
                    k = arrived_ref[pl.ds(p * page_rows, page_rows), lanes]
                    v = arrived_ref[pl.ds(CONTEXT_LENGTH + p * page_rows, page_rows), lanes]
                s = lax.dot_general(q, k, nt, preferred_element_type=f32) * scale
                w = jnp.where(lane_pos + p * page_rows < length, jnp.exp(s), 0.0)
                total = total + jnp.sum(w, axis=-1, keepdims=True)
                acc = acc + jnp.dot(w.astype(bf16), v, preferred_element_type=f32)
            out = acc / total
            for j in range(group):
                dec_rows[b][g * group + j] = out[j : j + 1]
    if arrived_only:
        row = jnp.concatenate(dec_rows[DEC_DEV - 1], axis=1)
        kept = base_ref[...].astype(f32)[: DEC_DEV - 1]
        o_ref[...] = jnp.concatenate([kept, row], axis=0).astype(o_ref.dtype)
        return
    dec_rows[DEC_DEV - 1] = [jnp.zeros((1, HEAD_SIZE), f32)] * QUERY_HEADS
    prefill_length = plen_ref[0]
    rows = group * PCH
    row_pos = lax.broadcasted_iota(jnp.int32, (rows, page_rows), 0) % PCH
    col_pos = lax.broadcasted_iota(jnp.int32, (rows, page_rows), 1)
    causal = col_pos <= row_pos
    for g in range(KEY_VALUE_HEADS):
        lanes = pl.ds(g * HEAD_SIZE, HEAD_SIZE)
        q = jnp.concatenate(
            [q_ref[:, pl.ds((g * group + j) * HEAD_SIZE, HEAD_SIZE)].astype(f32)[DEC_DEV:] for j in range(group)],
            axis=0,
        ).astype(bf16)
        kb = fk_ref[:, lanes].astype(f32)[DEC_DEV:].astype(bf16)
        vb = fv_ref[:, lanes].astype(f32)[DEC_DEV:].astype(bf16)
        s = lax.dot_general(q, kb, nt, preferred_element_type=f32) * scale
        w = jnp.where(causal, jnp.exp(s), 0.0)
        total = jnp.sum(w, axis=-1, keepdims=True)
        acc = jnp.dot(w.astype(bf16), vb, preferred_element_type=f32)
        for p in range(pages):
            page = pt_ref[0, p]
            k = pk_ref[page, :, lanes]
            v = pv_ref[page, :, lanes]
            s = lax.dot_general(q, k, nt, preferred_element_type=f32) * scale
            w = jnp.where(col_pos + p * page_rows < prefill_length, jnp.exp(s), 0.0)
            total = total + jnp.sum(w, axis=-1, keepdims=True)
            acc = acc + jnp.dot(w.astype(bf16), v, preferred_element_type=f32)
        out = acc / total
        for j in range(group):
            h = g * group + j
            dec_col = jnp.concatenate([dec_rows[b][h] for b in range(DEC_DEV)], axis=0)
            o_ref[:, pl.ds(h * HEAD_SIZE, HEAD_SIZE)] = jnp.concatenate(
                [dec_col, out[j * PCH : (j + 1) * PCH]], axis=0
            ).astype(o_ref.dtype)


def paged_attention(arrived_only, decode_table, prefill_table, decode_len, prefill_len, queries, fresh_keys, fresh_values, paged_keys, paged_values, arrived):
    smem = pl.BlockSpec(memory_space=pltpu.SMEM)
    vmem = pl.BlockSpec(memory_space=pltpu.VMEM)
    rows = 1 if arrived_only else queries.shape[0]
    return pl.pallas_call(
        functools.partial(attention_kernel, arrived_only),
        out_shape=jax.ShapeDtypeStruct((rows, queries.shape[1]), queries.dtype),
        in_specs=[smem] * 4 + [vmem] * 6,
        out_specs=vmem,
    )(decode_table, prefill_table, decode_len, prefill_len, queries, fresh_keys, fresh_values, paged_keys, paged_values, arrived)


def last_request_kernel(dl_ref, q_ref, fk_ref, fv_ref, arrived_ref, base_ref, o_ref):
    attention_kernel(
        True, None, None, dl_ref, None, q_ref, fk_ref, fv_ref, None, None, arrived_ref, o_ref, base_ref
    )


def last_request_attention(decode_len, queries, fresh_keys, fresh_values, arrived, base):
    def rows_of(width):
        return pl.BlockSpec((DEC_DEV, width), lambda i: (0, 0))

    return pl.pallas_call(
        last_request_kernel,
        out_shape=jax.ShapeDtypeStruct(base.shape, base.dtype),
        grid=(1,),
        in_specs=[
            pl.BlockSpec(memory_space=pltpu.SMEM),
            rows_of(queries.shape[1]),
            rows_of(fresh_keys.shape[1]),
            rows_of(fresh_values.shape[1]),
            pl.BlockSpec(arrived.shape, lambda i: (0, 0)),
            rows_of(base.shape[1]),
        ],
        out_specs=rows_of(base.shape[1]),
        input_output_aliases={5: 0},
    )(decode_len, queries, fresh_keys, fresh_values, arrived, base)


def capacity_for(token_count, route_count, expert_count):
    return min(token_count, (token_count * route_count // expert_count * 3 // 2 + 7) // 8 * 8)


def page_lookup(table, pool_flat):
    pool_count = pool_flat.shape[0]
    selector = (table[..., None] == jnp.arange(pool_count, dtype=jnp.int32)).astype(jnp.bfloat16)
    return jnp.einsum(
        "...p,pk->...k", selector, pool_flat, preferred_element_type=jnp.float32
    ).astype(jnp.bfloat16)


def on_device(
    queries,
    fresh_keys,
    fresh_values,
    residual,
    norm_gain,
    out_weight,
    router_weight,
    gate_weight,
    up_weight,
    down_weight,
    expert_ids,
    paged_keys,
    paged_values,
    decode_table,
    prefill_table,
    decode_len,
    prefill_len,
    departing_keys,
    departing_values,
    destination,
):
    width_total = KEY_VALUE_HEADS * HEAD_SIZE
    target_row = destination[0]
    dp_count = target_row.shape[0]
    rows_total = departing_keys.shape[1]
    chunk_rows = rows_total // dp_count
    both = jnp.concatenate([departing_keys[0], departing_values[0]], axis=0)
    both = both.reshape(dp_count, 2 * chunk_rows, width_total)
    spread = lax.all_to_all(both, "dp", split_axis=0, concat_axis=0, tiled=True)
    sources = jnp.sum(
        jnp.where(
            target_row[None, :] == jnp.arange(dp_count, dtype=jnp.int32)[:, None],
            jnp.arange(dp_count, dtype=jnp.int32)[None, :],
            0,
        ),
        axis=1,
    )
    routed = jnp.take(spread, sources, axis=0)
    gathered = lax.all_to_all(routed, "dp", split_axis=0, concat_axis=0, tiled=True)
    gathered = gathered.reshape(2 * rows_total, width_total)
    take_keys = gathered[None, :rows_total]
    take_values = gathered[None, rows_total:]
    token_count = queries.shape[0]
    table_args = (decode_table, prefill_table, decode_len, prefill_len, queries, fresh_keys, fresh_values)
    attended = paged_attention(False, *table_args, paged_keys, paged_values, fresh_keys)
    attended = last_request_attention(decode_len, queries, fresh_keys, fresh_values, gathered, attended)
    hidden = residual.astype(jnp.float32) + jnp.dot(
        attended, out_weight, preferred_element_type=jnp.float32
    )
    variance = jnp.mean(hidden * hidden, axis=-1, keepdims=True)
    normed = (hidden * lax.rsqrt(variance + 1e-06) * norm_gain).astype(jnp.bfloat16)
    logits = jnp.dot(normed, router_weight, preferred_element_type=jnp.float32)
    expert_count = router_weight.shape[1]
    expert_range = jnp.arange(expert_count, dtype=jnp.int32)
    chosen = jnp.sum(
        jnp.where(expert_ids[:, :, None] == expert_range, logits[:, None, :], 0.0), axis=-1
    )
    chosen = jax.nn.sigmoid(chosen)
    gates = chosen / jnp.sum(chosen, axis=1, keepdims=True)
    route_count = expert_ids.shape[1]
    capacity = capacity_for(token_count, route_count, expert_count)
    slot_total = expert_count * capacity
    flat_ids = expert_ids.T.reshape(-1)
    hits = (flat_ids[:, None] == expert_range[None, :]).astype(jnp.int32)
    ranks = jnp.sum((jnp.cumsum(hits, axis=0) - 1) * hits, axis=1)
    slot_of_route = flat_ids * capacity + ranks
    route_slots = (
        slot_of_route[:, None] == jnp.arange(slot_total, dtype=jnp.int32)[None, :]
    ).astype(jnp.bfloat16)
    token_slots = jnp.sum(route_slots.reshape(route_count, token_count, slot_total), axis=0)
    outgoing = jnp.einsum(
        "ts,td->sd", token_slots, normed, preferred_element_type=jnp.float32
    ).astype(jnp.bfloat16)
    outgoing = outgoing.reshape(expert_count, capacity, normed.shape[1])
    received = lax.all_to_all(outgoing, "expert", split_axis=0, concat_axis=0, tiled=True)
    gate_part = jnp.einsum(
        "scd,df->scf", received, gate_weight[0], preferred_element_type=jnp.float32
    )
    up_part = jnp.einsum("scd,df->scf", received, up_weight[0], preferred_element_type=jnp.float32)
    inner = lax.optimization_barrier((jax.nn.relu(gate_part) * up_part).astype(jnp.bfloat16))
    processed = jnp.einsum(
        "scf,fd->scd", inner, down_weight[0], preferred_element_type=jnp.float32
    ).astype(jnp.bfloat16)
    returned = lax.all_to_all(processed, "expert", split_axis=0, concat_axis=0, tiled=True)
    returned_flat = returned.reshape(slot_total, returned.shape[2])
    route_out = jnp.dot(route_slots, returned_flat, preferred_element_type=jnp.float32).astype(
        jnp.bfloat16
    ).reshape(route_count, token_count, -1)
    mixture = jnp.sum(gates.T[:, :, None] * route_out.astype(jnp.float32), axis=0)
    layer_out = (hidden + mixture).astype(jnp.bfloat16)
    last_len = decode_len[0, DEC_DEV - 1]
    moved_keys = lax.dynamic_update_slice(
        take_keys,
        fresh_keys[DEC_DEV - 1][None, None],
        (jnp.zeros((), jnp.int32), last_len, jnp.zeros((), jnp.int32)),
    )
    moved_values = lax.dynamic_update_slice(
        take_values,
        fresh_values[DEC_DEV - 1][None, None],
        (jnp.zeros((), jnp.int32), last_len, jnp.zeros((), jnp.int32)),
    )
    return (layer_out, moved_keys, moved_values)


def solution(mesh):
    return jax.shard_map(
        on_device,
        mesh=mesh,
        in_specs=(
            P(("dp", "expert"), None),
            P(("dp", "expert"), None),
            P(("dp", "expert"), None),
            P(("dp", "expert"), None),
            P(),
            P(),
            P(),
            P("expert", None, None),
            P("expert", None, None),
            P("expert", None, None),
            P(("dp", "expert"), None),
            P(("dp", "expert"), None, None),
            P(("dp", "expert"), None, None),
            P(("dp", "expert"), None),
            P(("dp", "expert"), None),
            P(("dp", "expert"), None),
            P(("dp", "expert")),
            P(("dp", "expert"), None, None),
            P(("dp", "expert"), None, None),
            P("expert", None),
        ),
        out_specs=(
            P(("dp", "expert"), None),
            P(("dp", "expert"), None, None),
            P(("dp", "expert"), None, None),
        ),
        check_vma=False,
    )
```

```python
import functools

import jax
import jax.numpy as jnp
from jax import lax
from jax.experimental import pallas as pl
from jax.experimental.pallas import tpu as pltpu
from jax.sharding import PartitionSpec as P

QUERY_HEADS = 12
KEY_VALUE_HEADS = 2
HEAD_SIZE = 128
DEC_DEV = 8
PCH = 128
CONTEXT_LENGTH = 512
PAGE_TOKENS = 128


def attention_kernel(arrived_only, dt_ref, pt_ref, dl_ref, plen_ref, q_ref, fk_ref, fv_ref, pk_ref, pv_ref, arrived_ref, o_ref, base_ref=None):
    f32 = jnp.float32
    bf16 = jnp.bfloat16
    group = QUERY_HEADS // KEY_VALUE_HEADS
    scale = HEAD_SIZE ** (-0.5)
    page_rows = PAGE_TOKENS if pk_ref is None else pk_ref.shape[1]
    pages = CONTEXT_LENGTH // page_rows
    nt = (((1,), (1,)), ((), ()))
    lane_pos = lax.broadcasted_iota(jnp.int32, (1, page_rows), 1)
    dec_rows = [[None] * QUERY_HEADS for _ in range(DEC_DEV)]
    requests = [DEC_DEV - 1] if arrived_only else list(range(DEC_DEV - 1))
    for g in range(KEY_VALUE_HEADS):
        lanes = pl.ds(g * HEAD_SIZE, HEAD_SIZE)
        for b in requests:
            length = dl_ref[0, b]
            q = jnp.concatenate(
                [q_ref[pl.ds(b, 1), pl.ds((g * group + j) * HEAD_SIZE, HEAD_SIZE)] for j in range(group)],
                axis=0,
            )
            kf = fk_ref[pl.ds(b, 1), lanes].astype(f32)
            vf = fv_ref[pl.ds(b, 1), lanes].astype(f32)
            w_new = jnp.exp(jnp.sum(q.astype(f32) * kf, axis=-1, keepdims=True) * scale)
            total = w_new
            acc = w_new.astype(bf16).astype(f32) * vf
            for p in range(pages):
                if b < DEC_DEV - 1:
                    page = dt_ref[b, p]
                    k = pk_ref[page, :, lanes]
                    v = pv_ref[page, :, lanes]
                else:
                    k = arrived_ref[pl.ds(p * page_rows, page_rows), lanes]
                    v = arrived_ref[pl.ds(p * page_rows, page_rows), pl.ds(KEY_VALUE_HEADS * HEAD_SIZE + g * HEAD_SIZE, HEAD_SIZE)]
                s = lax.dot_general(q, k, nt, preferred_element_type=f32) * scale
                w = jnp.where(lane_pos + p * page_rows < length, jnp.exp(s), 0.0)
                total = total + jnp.sum(w, axis=-1, keepdims=True)
                acc = acc + jnp.dot(w.astype(bf16), v, preferred_element_type=f32)
            out = acc / total
            for j in range(group):
                dec_rows[b][g * group + j] = out[j : j + 1]
    if arrived_only:
        row = jnp.concatenate(dec_rows[DEC_DEV - 1], axis=1)
        kept = base_ref[...].astype(f32)[: DEC_DEV - 1]
        o_ref[...] = jnp.concatenate([kept, row], axis=0).astype(o_ref.dtype)
        return
    dec_rows[DEC_DEV - 1] = [jnp.zeros((1, HEAD_SIZE), f32)] * QUERY_HEADS
    prefill_length = plen_ref[0]
    rows = group * PCH
    row_pos = lax.broadcasted_iota(jnp.int32, (rows, page_rows), 0) % PCH
    col_pos = lax.broadcasted_iota(jnp.int32, (rows, page_rows), 1)
    causal = col_pos <= row_pos
    for g in range(KEY_VALUE_HEADS):
        lanes = pl.ds(g * HEAD_SIZE, HEAD_SIZE)
        q = jnp.concatenate(
            [q_ref[:, pl.ds((g * group + j) * HEAD_SIZE, HEAD_SIZE)].astype(f32)[DEC_DEV:] for j in range(group)],
            axis=0,
        ).astype(bf16)
        kb = fk_ref[:, lanes].astype(f32)[DEC_DEV:].astype(bf16)
        vb = fv_ref[:, lanes].astype(f32)[DEC_DEV:].astype(bf16)
        s = lax.dot_general(q, kb, nt, preferred_element_type=f32) * scale
        w = jnp.where(causal, jnp.exp(s), 0.0)
        total = jnp.sum(w, axis=-1, keepdims=True)
        acc = jnp.dot(w.astype(bf16), vb, preferred_element_type=f32)
        for p in range(pages):
            page = pt_ref[0, p]
            k = pk_ref[page, :, lanes]
            v = pv_ref[page, :, lanes]
            s = lax.dot_general(q, k, nt, preferred_element_type=f32) * scale
            w = jnp.where(col_pos + p * page_rows < prefill_length, jnp.exp(s), 0.0)
            total = total + jnp.sum(w, axis=-1, keepdims=True)
            acc = acc + jnp.dot(w.astype(bf16), v, preferred_element_type=f32)
        out = acc / total
        for j in range(group):
            h = g * group + j
            dec_col = jnp.concatenate([dec_rows[b][h] for b in range(DEC_DEV)], axis=0)
            o_ref[:, pl.ds(h * HEAD_SIZE, HEAD_SIZE)] = jnp.concatenate(
                [dec_col, out[j * PCH : (j + 1) * PCH]], axis=0
            ).astype(o_ref.dtype)


def paged_attention(arrived_only, decode_table, prefill_table, decode_len, prefill_len, queries, fresh_keys, fresh_values, paged_keys, paged_values, arrived):
    smem = pl.BlockSpec(memory_space=pltpu.SMEM)
    vmem = pl.BlockSpec(memory_space=pltpu.VMEM)
    rows = 1 if arrived_only else queries.shape[0]
    return pl.pallas_call(
        functools.partial(attention_kernel, arrived_only),
        out_shape=jax.ShapeDtypeStruct((rows, queries.shape[1]), queries.dtype),
        in_specs=[smem] * 4 + [vmem] * 6,
        out_specs=vmem,
    )(decode_table, prefill_table, decode_len, prefill_len, queries, fresh_keys, fresh_values, paged_keys, paged_values, arrived)


def last_request_kernel(dl_ref, q_ref, fk_ref, fv_ref, arrived_ref, base_ref, o_ref):
    attention_kernel(
        True, None, None, dl_ref, None, q_ref, fk_ref, fv_ref, None, None, arrived_ref, o_ref, base_ref
    )


def last_request_attention(decode_len, queries, fresh_keys, fresh_values, arrived, base):
    def rows_of(width):
        return pl.BlockSpec((DEC_DEV, width), lambda i: (0, 0))

    return pl.pallas_call(
        last_request_kernel,
        out_shape=jax.ShapeDtypeStruct(base.shape, base.dtype),
        grid=(1,),
        in_specs=[
            pl.BlockSpec(memory_space=pltpu.SMEM),
            rows_of(queries.shape[1]),
            rows_of(fresh_keys.shape[1]),
            rows_of(fresh_values.shape[1]),
            pl.BlockSpec(arrived.shape, lambda i: (0, 0)),
            rows_of(base.shape[1]),
        ],
        out_specs=rows_of(base.shape[1]),
        input_output_aliases={5: 0},
    )(decode_len, queries, fresh_keys, fresh_values, arrived, base)


def capacity_for(token_count, route_count, expert_count):
    return min(token_count, (token_count * route_count // expert_count * 3 // 2 + 7) // 8 * 8)


def page_lookup(table, pool_flat):
    pool_count = pool_flat.shape[0]
    selector = (table[..., None] == jnp.arange(pool_count, dtype=jnp.int32)).astype(jnp.bfloat16)
    return jnp.einsum(
        "...p,pk->...k", selector, pool_flat, preferred_element_type=jnp.float32
    ).astype(jnp.bfloat16)


def on_device(
    queries,
    fresh_keys,
    fresh_values,
    residual,
    norm_gain,
    out_weight,
    router_weight,
    gate_weight,
    up_weight,
    down_weight,
    expert_ids,
    paged_keys,
    paged_values,
    decode_table,
    prefill_table,
    decode_len,
    prefill_len,
    departing_keys,
    departing_values,
    destination,
):
    width_total = KEY_VALUE_HEADS * HEAD_SIZE
    target_row = destination[0]
    dp_count = target_row.shape[0]
    rows_total = departing_keys.shape[1]
    chunk_rows = rows_total // dp_count
    both = jnp.concatenate([departing_keys[0], departing_values[0]], axis=-1)
    both = both.reshape(dp_count, chunk_rows, 2 * width_total)
    spread = lax.all_to_all(both, "dp", split_axis=0, concat_axis=0, tiled=True)
    sources = jnp.sum(
        jnp.where(
            target_row[None, :] == jnp.arange(dp_count, dtype=jnp.int32)[:, None],
            jnp.arange(dp_count, dtype=jnp.int32)[None, :],
            0,
        ),
        axis=1,
    )
    routed = jnp.take(spread, sources, axis=0)
    gathered = lax.all_to_all(routed, "dp", split_axis=0, concat_axis=0, tiled=True)
    gathered = gathered.reshape(rows_total, 2 * width_total)
    take_keys = gathered[None, :, :width_total]
    take_values = gathered[None, :, width_total:]
    token_count = queries.shape[0]
    table_args = (decode_table, prefill_table, decode_len, prefill_len, queries, fresh_keys, fresh_values)
    attended = paged_attention(False, *table_args, paged_keys, paged_values, both)
    attended_rows = last_request_attention(
        decode_len, queries, fresh_keys, fresh_values, gathered, attended[:DEC_DEV]
    )
    hidden = residual.astype(jnp.float32) + jnp.dot(
        attended, out_weight, preferred_element_type=jnp.float32
    )
    last_row = DEC_DEV - 1
    hidden_row = residual[last_row : last_row + 1].astype(jnp.float32) + jnp.dot(
        attended_rows[last_row : last_row + 1], out_weight, preferred_element_type=jnp.float32
    )
    hidden = lax.dynamic_update_slice(hidden, hidden_row, (last_row, 0))
    variance = jnp.mean(hidden * hidden, axis=-1, keepdims=True)
    normed = (hidden * lax.rsqrt(variance + 1e-06) * norm_gain).astype(jnp.bfloat16)
    logits = jnp.dot(normed, router_weight, preferred_element_type=jnp.float32)
    expert_count = router_weight.shape[1]
    expert_range = jnp.arange(expert_count, dtype=jnp.int32)
    chosen = jnp.sum(
        jnp.where(expert_ids[:, :, None] == expert_range, logits[:, None, :], 0.0), axis=-1
    )
    chosen = jax.nn.sigmoid(chosen)
    gates = chosen / jnp.sum(chosen, axis=1, keepdims=True)
    route_count = expert_ids.shape[1]
    capacity = capacity_for(token_count, route_count, expert_count)
    slot_total = expert_count * capacity
    flat_ids = expert_ids.T.reshape(-1)
    hits = (flat_ids[:, None] == expert_range[None, :]).astype(jnp.int32)
    ranks = jnp.sum((jnp.cumsum(hits, axis=0) - 1) * hits, axis=1)
    slot_of_route = flat_ids * capacity + ranks
    route_slots = (
        slot_of_route[:, None] == jnp.arange(slot_total, dtype=jnp.int32)[None, :]
    ).astype(jnp.bfloat16)
    token_slots = jnp.sum(route_slots.reshape(route_count, token_count, slot_total), axis=0)
    outgoing = jnp.einsum(
        "ts,td->sd", token_slots, normed, preferred_element_type=jnp.float32
    ).astype(jnp.bfloat16)
    outgoing = outgoing.reshape(expert_count, capacity, normed.shape[1])
    received = lax.all_to_all(outgoing, "expert", split_axis=0, concat_axis=0, tiled=True)
    gate_part = jnp.einsum(
        "scd,df->scf", received, gate_weight[0], preferred_element_type=jnp.float32
    )
    up_part = jnp.einsum("scd,df->scf", received, up_weight[0], preferred_element_type=jnp.float32)
    inner = lax.optimization_barrier((jax.nn.relu(gate_part) * up_part).astype(jnp.bfloat16))
    processed = jnp.einsum(
        "scf,fd->scd", inner, down_weight[0], preferred_element_type=jnp.float32
    ).astype(jnp.bfloat16)
    returned = lax.all_to_all(processed, "expert", split_axis=0, concat_axis=0, tiled=True)
    returned_flat = returned.reshape(slot_total, returned.shape[2])
    route_out = jnp.dot(route_slots, returned_flat, preferred_element_type=jnp.float32).astype(
        jnp.bfloat16
    ).reshape(route_count, token_count, -1)
    mixture = jnp.sum(gates.T[:, :, None] * route_out.astype(jnp.float32), axis=0)
    layer_out = (hidden + mixture).astype(jnp.bfloat16)
    last_len = decode_len[0, DEC_DEV - 1]
    moved_keys = lax.dynamic_update_slice(
        take_keys,
        fresh_keys[DEC_DEV - 1][None, None],
        (jnp.zeros((), jnp.int32), last_len, jnp.zeros((), jnp.int32)),
    )
    moved_values = lax.dynamic_update_slice(
        take_values,
        fresh_values[DEC_DEV - 1][None, None],
        (jnp.zeros((), jnp.int32), last_len, jnp.zeros((), jnp.int32)),
    )
    return (layer_out, moved_keys, moved_values)


def solution(mesh):
    return jax.shard_map(
        on_device,
        mesh=mesh,
        in_specs=(
            P(("dp", "expert"), None),
            P(("dp", "expert"), None),
            P(("dp", "expert"), None),
            P(("dp", "expert"), None),
            P(),
            P(),
            P(),
            P("expert", None, None),
            P("expert", None, None),
            P("expert", None, None),
            P(("dp", "expert"), None),
            P(("dp", "expert"), None, None),
            P(("dp", "expert"), None, None),
            P(("dp", "expert"), None),
            P(("dp", "expert"), None),
            P(("dp", "expert"), None),
            P(("dp", "expert")),
            P(("dp", "expert"), None, None),
            P(("dp", "expert"), None, None),
            P("expert", None),
        ),
        out_specs=(
            P(("dp", "expert"), None),
            P(("dp", "expert"), None, None),
            P(("dp", "expert"), None, None),
        ),
        check_vma=False,
    )
```
